32 devices in a mesh: angle: 4 (over y, core), row: 8 (over z, x).
Axes of the slice: x: 2, y: 2, z: 4, core: 2. Of those that a mesh axis runs over, the one named last changes fastest.
Arguments:
- projections: float32 [32, 512, 2048], P('angle', 'row')
- mean_flat: float32 [512, 2048], P('row')
- eigen_flats: float32 [20, 512, 2048], P(None, 'row')
- stretch: int32 [32], P('angle'), may hold values from 96 to 128
- offset: int32 [32], P('angle'), may hold values from 0 to 128
- tilt_shift: int32 [32], P('angle'), may hold values from 0 to 128, as said below
Outputs:
- volume: float32 [512, 2048], P('row', 'angle')
The draws below stay inside these ranges and needn't reach their ends.
Inputs may be any that keep to these rules, and one draw needn't show every extreme that they name: `tilt_shift`: every draw has some projection with shift 2 * 64.
All inputs are finite; a program needn't handle non-finite values.
Results may differ from the reference program's by a relative error of at most 0.0034.
Values sent between devices are 32-bit elements; how exact they have to be, the bound alone decides.
No kernel may reach another device: no remote copies, remote signals or barrier semaphores. Data moves between devices by JAX's collectives and lax.ppermute only.
A program may use at most 128 MiB of HBM per device.

```python
import math
import jax
import jax.numpy as jnp
from jax import lax

W = 2048
K = 20
TILE = 128
STRIDE = 4
RD = 64
R = 512
NP = 32


def flat_parts(key):
    base_key = jax.random.fold_in(key, 11)
    key_mean = jax.random.fold_in(base_key, 0)
    key_shape = jax.random.fold_in(base_key, 1)
    key_common = jax.random.fold_in(base_key, 3)
    key_load = jax.random.fold_in(base_key, 4)
    mean_part = jax.random.uniform(key_mean, (R, W), jnp.float32, 1.0, 3.0)
    rising = 0.6 * 3.0 ** (jnp.arange(R, dtype=jnp.float32) / R)
    shape_part = jax.random.normal(key_shape, (K, R, W), jnp.float32)
    common_part = jax.random.normal(key_common, (R, W), jnp.float32)
    loadings = jax.random.uniform(key_load, (K,), jnp.float32, 0.4, 1.0)
    mixed_part = shape_part + loadings[:, None, None] * common_part[None]
    eigen_part = mixed_part * rising[None, :, None]
    return (mean_part, eigen_part)


def object_part(key):
    key_amp, key_half, key_center, key_swing, key_phase, key_rows = jax.random.split(jax.random.fold_in(key, 53), 6)
    amounts = jax.random.uniform(key_amp, (3,), jnp.float32, 5.0, 9.0)
    halves = jax.random.uniform(key_half, (3,), jnp.float32, 0.15, 0.3) * W
    centers = jax.random.uniform(key_center, (3,), jnp.float32, 0.4, 0.6) * W
    swings = jax.random.uniform(key_swing, (3,), jnp.float32, 0.05, 0.15) * W
    phases = jax.random.uniform(key_phase, (3,), jnp.float32, 0.0, 2.0 * math.pi)
    angles = jnp.arange(NP, dtype=jnp.float32) * (math.pi / NP)
    centre_now = centers[None, :] + swings[None, :] * jnp.cos(angles[:, None] + phases[None, :])
    columns = jnp.arange(W, dtype=jnp.float32)
    spread = (columns[None, None, :] - centre_now[:, :, None]) / halves[None, :, None]
    chords = amounts[None, :, None] * jnp.sqrt(jnp.maximum(1.0 - spread * spread, 0.0))
    profile = chords[:, 0] + chords[:, 1] + chords[:, 2]
    row_phase = jax.random.uniform(key_rows, (), jnp.float32, 0.0, 2.0 * math.pi)
    row_factor = 1.0 + 0.25 * jnp.sin(2.0 * math.pi * jnp.arange(R, dtype=jnp.float32) / R + row_phase)
    return profile[:, None, :] * row_factor[None, :, None]


def texture_part(key):
    key_amp, key_period, key_phase = jax.random.split(jax.random.fold_in(key, 67), 3)
    strengths = jax.random.uniform(key_amp, (8, NP, R), jnp.float32, 3.0, 6.0)
    periods = jnp.exp(jax.random.uniform(key_period, (8, NP), jnp.float32, math.log(40.0), math.log(160.0)))
    frequency = 1.0 / periods
    phases = jax.random.uniform(key_phase, (8, NP, R), jnp.float32, 0.0, 2.0 * math.pi)
    columns = jnp.arange(W, dtype=jnp.float32)
    total = jnp.zeros((NP, R, W), jnp.float32)
    for which in range(8):
        cycles = columns[None, :] * frequency[which][:, None]
        cycles = cycles - jnp.floor(cycles)
        wave = jnp.sin(2.0 * math.pi * cycles[:, None, :] + phases[which][:, :, None])
        total = total + strengths[which][:, :, None] * wave
    return total


def draw_mean_flat(key, part):
    return flat_parts(key)[0]


def draw_eigen_flats(key, part):
    return flat_parts(key)[1]


def draw_projections(key, part):
    mean_part, eigen_part = flat_parts(key)
    key_coef, key_rough, key_local = jax.random.split(jax.random.fold_in(key, 29), 3)
    common = jax.random.normal(key_coef, (NP, K), jnp.float32)
    rough = jax.random.normal(key_rough, (NP, R, W), jnp.float32)
    local = 0.5 * jax.random.normal(key_local, (NP, K, R), jnp.float32)
    row_weights = common[:, :, None] + local
    flat_part = jnp.einsum('pkr,krc->prc', row_weights, eigen_part)
    return mean_part[None] + flat_part - object_part(key) - texture_part(key) + rough


def draw_tilt_shift(key, part):
    key_shift, key_pick = jax.random.split(jax.random.fold_in(key, 41))
    shifts = jax.random.randint(key_shift, (NP,), 0, 2 * RD + 1, dtype=jnp.int32)
    chosen = jax.random.randint(key_pick, (), 0, NP, dtype=jnp.int32)
    return jnp.where(jnp.arange(NP, dtype=jnp.int32) == chosen, jnp.int32(2 * RD), shifts)


def plant(drawn, rng, smallest, top_value):
    longest = drawn.shape.index(max(drawn.shape))
    spots = []
    for shift in (0, 1):
        where = [jax.random.randint(jax.random.fold_in(rng, axis), (), 0, length) for axis, length in enumerate(drawn.shape)]
        where[longest] = (where[longest] + shift) % drawn.shape[longest]
        spots.append(tuple(where))
    return drawn.at[spots[0]].set(smallest).at[spots[1]].set(top_value)


def setup_inputs(seed: int = 0) -> dict:
    streams_of = jax.random.split(jax.random.key(seed), 7)
    projections = draw_projections(jax.random.fold_in(streams_of[6], 71), 0)
    mean_flat = draw_mean_flat(jax.random.fold_in(streams_of[6], 71), 0)
    eigen_flats = draw_eigen_flats(jax.random.fold_in(streams_of[6], 71), 0)
    stretch = plant(jax.random.randint(streams_of[3], (NP,), 96, 129), jax.random.fold_in(streams_of[3], 1), 96, 128).astype(jnp.int32)
    offset = plant(jax.random.randint(streams_of[4], (NP,), 0, 129), jax.random.fold_in(streams_of[4], 1), 0, 128).astype(jnp.int32)
    tilt_shift = draw_tilt_shift(jax.random.fold_in(streams_of[6], 71), 0)
    return {"projections": projections, "mean_flat": mean_flat, "eigen_flats": eigen_flats, "stretch": stretch, "offset": offset, "tilt_shift": tilt_shift}


def ramp_table(col_count):
    index_cols = jnp.arange(col_count, dtype=jnp.int32)
    col_offset = index_cols[None, :] - index_cols[:, None]
    odd_offset = col_offset % 2 != 0
    distance = col_offset.astype(jnp.float32)
    safe_dist = jnp.where(odd_offset, distance, jnp.ones_like(distance))
    values = jnp.where(odd_offset, -1.0 / (math.pi * math.pi * safe_dist * safe_dist), jnp.zeros_like(distance))
    return jnp.where(col_offset == 0, jnp.full_like(distance, 0.25), values)

def hat_tiles(stretch_one, offset_one, col_count):
    tile_count = col_count // TILE
    tile_ids = jnp.arange(tile_count, dtype=jnp.int32)
    inner = jnp.arange(TILE, dtype=jnp.int32)
    voxels = tile_ids[:, None] * TILE + inner[None, :]
    scaled = voxels * stretch_one
    columns = scaled // TILE + offset_one
    fraction = (scaled % TILE).astype(jnp.float32) / TILE
    window_lo = tile_ids * stretch_one + offset_one
    relative = columns - window_lo[:, None]
    window = jnp.arange(2 * TILE, dtype=jnp.int32)
    first_hit = window[None, :, None] == relative[:, None, :]
    second_hit = window[None, :, None] == relative[:, None, :] + 1
    zeros_like = jnp.zeros((tile_count, 2 * TILE, TILE), jnp.float32)
    hat_weights = jnp.where(first_hit, (1.0 - fraction)[:, None, :], zeros_like) + jnp.where(second_hit, fraction[:, None, :], zeros_like)
    return (window_lo, hat_weights)

def backproject(filtered, stretch_one, offset_one):
    row_count, col_count = filtered.shape
    padded = jnp.pad(filtered, ((0, 0), (0, 2 * TILE)))
    window_lo, hat_weights = hat_tiles(stretch_one, offset_one, col_count)
    windows = jax.vmap(lambda lo_col: lax.dynamic_slice_in_dim(padded, lo_col, 2 * TILE, 1))(window_lo)
    image = jnp.einsum('trc,tcx->rtx', windows.astype(jnp.float32), hat_weights.astype(jnp.float32))
    return image.reshape(row_count, col_count)

def reference(projections, mean_flat, eigen_flats, stretch, offset, tilt_shift):
    sampled = eigen_flats.reshape(K, R // STRIDE, STRIDE, W)[:, :, 0, :]
    targets = (projections - mean_flat[None]).reshape(NP, R // STRIDE, STRIDE, W)[:, :, 0, :]
    gram_matrix = jnp.einsum('krc,lrc->kl', sampled, sampled, precision=lax.Precision.HIGHEST)
    gram_matrix = gram_matrix + W * jnp.eye(K, dtype=jnp.float32)
    rhs_matrix = jnp.einsum('krc,prc->kp', sampled, targets, precision=lax.Precision.HIGHEST)
    cholesky_factor = jnp.linalg.cholesky(gram_matrix)
    middle = lax.linalg.triangular_solve(cholesky_factor, rhs_matrix, left_side=True, lower=True)
    solved = lax.linalg.triangular_solve(cholesky_factor, middle, left_side=True, lower=True, transpose_a=True)
    flat_weights = solved.T
    filter_table = ramp_table(W)

    def deposit_one(proj_id, layers):
        weight_row = lax.dynamic_index_in_dim(flat_weights, proj_id, 0, keepdims=False)
        measured = lax.dynamic_index_in_dim(projections, proj_id, 0, keepdims=False)
        flat_now = mean_flat + jnp.einsum('k,krc->rc', weight_row, eigen_flats, precision=lax.Precision.HIGHEST)
        absorb = flat_now - measured
        filtered = jnp.dot(absorb.astype(jnp.float32), filter_table.astype(jnp.float32), precision=lax.Precision.HIGHEST, preferred_element_type=jnp.float32).astype(jnp.bfloat16)
        stretch_one = lax.dynamic_index_in_dim(stretch, proj_id, 0, keepdims=False).astype(jnp.int32)
        offset_one = lax.dynamic_index_in_dim(offset, proj_id, 0, keepdims=False).astype(jnp.int32)
        image = backproject(filtered, stretch_one, offset_one)
        start_row = lax.dynamic_index_in_dim(tilt_shift, proj_id, 0, keepdims=False).astype(jnp.int32)
        current = lax.dynamic_slice_in_dim(layers, start_row, R, 0)
        return lax.dynamic_update_slice_in_dim(layers, current + image, start_row, 0)
    layers = lax.fori_loop(0, NP, deposit_one, jnp.zeros((R + 2 * RD, W), jnp.float32))
    return layers[:R] / math.sqrt(NP)
```

```python
import math

import jax
import jax.numpy as jnp
from jax import lax
from jax.experimental import pallas as pl
from jax.experimental.pallas import tpu as pltpu
from jax.sharding import PartitionSpec as P

TILE = 128
STRIDE = 4
GROUP = 4
BLK = 256
CHUNK = 16


def shifted(value, axis, by):
    size = lax.axis_size(axis)
    pairs = [(i, i + by) for i in range(size) if 0 <= i + by < size]
    return lax.ppermute(value, axis, pairs)


def split_bf16(x):
    hi = x.astype(jnp.bfloat16)
    lo = (x - hi.astype(jnp.float32)).astype(jnp.bfloat16)
    return hi, lo


def half_table(half):
    idx = lax.optimization_barrier(jnp.arange(half, dtype=jnp.int32))
    dist = (2 * (idx[None, :] - idx[:, None]) + 1).astype(jnp.float32)
    table = -1.0 / (math.pi * math.pi * dist * dist)
    return split_bf16(table)


def block_perm():
    rows = jnp.arange(BLK, dtype=jnp.int32)[:, None]
    cols = jnp.arange(BLK, dtype=jnp.int32)[None, :]
    target = rows // 2 + (BLK // 2) * (rows % 2)
    perm = (cols == target).astype(jnp.bfloat16)
    return perm, perm.T


def dot(a, b):
    return jnp.dot(a, b, preferred_element_type=jnp.float32)


def dot_nt(a, b):
    return lax.dot_general(a, b, (((1,), (1,)), ((), ())), preferred_element_type=jnp.float32)


def main_kernel(w_ref, st_ref, off_ref, tilt_ref, proj_ref, mean_ref, e_ref, ghi_ref, glo_ref,
                perm_ref, permt_ref, out_ref, a_scr, fs_scr):
    g = pl.program_id(0)
    flat_count, row_count, col_count = e_ref.shape
    rows = GROUP * row_count
    half = col_count // 2
    nblk = col_count // BLK
    hb = BLK // 2
    tile_count = col_count // TILE

    @pl.when(g == 0)
    def _():
        out_ref[...] = jnp.zeros_like(out_ref)

    for q in range(GROUP):
        p = g * GROUP + q
        wk = [w_ref[p, k] for k in range(flat_count)]

        def absorb_chunk(c, carry):
            r0 = pl.multiple_of(c * CHUNK, CHUNK)
            acc = mean_ref[pl.ds(r0, CHUNK), :] - proj_ref[q, pl.ds(r0, CHUNK), :]
            for k in range(flat_count):
                acc = acc + wk[k] * e_ref[k, pl.ds(r0, CHUNK), :]
            a_scr[pl.ds(q * row_count + r0, CHUNK), :] = acc
            return carry

        lax.fori_loop(0, row_count // CHUNK, absorb_chunk, 0)

    perm = perm_ref[...]
    even_hi, even_lo, odd_hi, odd_lo = [], [], [], []
    for b in range(nblk):
        blk = a_scr[:, b * BLK:(b + 1) * BLK]
        hi, lo = split_bf16(blk)
        ph = dot(hi, perm).astype(jnp.bfloat16)
        po = dot(lo, perm).astype(jnp.bfloat16)
        even_hi.append(ph[:, :hb])
        odd_hi.append(ph[:, hb:])
        even_lo.append(po[:, :hb])
        odd_lo.append(po[:, hb:])
    even_hi = jnp.concatenate(even_hi, axis=1)
    even_lo = jnp.concatenate(even_lo, axis=1)
    odd_hi = jnp.concatenate(odd_hi, axis=1)
    odd_lo = jnp.concatenate(odd_lo, axis=1)
    ghi = ghi_ref[...]
    glo = glo_ref[...]
    f_odd = dot(even_hi, ghi) + dot(even_lo, ghi) + dot(even_hi, glo)
    f_odd = f_odd + 0.25 * (odd_hi.astype(jnp.float32) + odd_lo.astype(jnp.float32))
    f_even = dot_nt(odd_hi, ghi) + dot_nt(odd_lo, ghi) + dot_nt(odd_hi, glo)
    f_even = f_even + 0.25 * (even_hi.astype(jnp.float32) + even_lo.astype(jnp.float32))
    fe = f_even.astype(jnp.bfloat16)
    fo = f_odd.astype(jnp.bfloat16)
    permt = permt_ref[...]
    nat = []
    for b in range(nblk):
        pair = jnp.concatenate([fe[:, b * hb:(b + 1) * hb], fo[:, b * hb:(b + 1) * hb]], axis=1)
        nat.append(dot(pair, permt).astype(jnp.bfloat16))
    filtered = jnp.concatenate(nat, axis=1)

    layer_rows = out_ref.shape[0]
    pad_cols = fs_scr.shape[1] - col_count
    fs_scr[:, col_count:] = jnp.zeros((layer_rows, pad_cols), jnp.bfloat16)
    z_iota = lax.broadcasted_iota(jnp.int32, (layer_rows, row_count), 0)
    r_iota = lax.broadcasted_iota(jnp.int32, (layer_rows, row_count), 1)
    w_iota = lax.broadcasted_iota(jnp.int32, (2 * TILE, TILE), 0)
    i_iota = lax.broadcasted_iota(jnp.int32, (1, TILE), 1)
    for q in range(GROUP):
        p = g * GROUP + q
        stretch_one = st_ref[p]
        offset_one = off_ref[p]
        tilt_one = tilt_ref[p]
        shift = (z_iota == r_iota + tilt_one).astype(jnp.bfloat16)
        fs = dot(shift, filtered[q * row_count:(q + 1) * row_count, :])
        fs_scr[:, :col_count] = fs.astype(jnp.bfloat16)
        scaled = i_iota * stretch_one
        rel = scaled // TILE
        frac = (scaled % TILE).astype(jnp.float32) / TILE

        def tile_body(t, carry):
            lo_col = t * stretch_one + offset_one
            blk_id = lo_col // TILE
            target = rel + (lo_col - blk_id * TILE)
            hat = jnp.where(w_iota == target, 1.0 - frac, 0.0) + jnp.where(w_iota == target + 1, frac, 0.0)
            start = pl.multiple_of(blk_id * TILE, TILE)
            window = fs_scr[:, pl.ds(start, 2 * TILE)]
            img = dot(window, hat.astype(jnp.bfloat16))
            c0 = pl.multiple_of(t * TILE, TILE)
            out_ref[:, pl.ds(c0, TILE)] += img
            return carry

        lax.fori_loop(0, tile_count, tile_body, 0)


def deposit(flat_weights, stretch, offset, tilt_shift, projections, mean_flat, eigen_flats):
    proj_count, row_count, col_count = projections.shape
    flat_count = eigen_flats.shape[0]
    half = col_count // 2
    ghi, glo = half_table(half)
    perm, permt = block_perm()
    smem = pl.BlockSpec(memory_space=pltpu.SMEM)
    once = dict(pipeline_mode=pl.Buffered(1))
    return pl.pallas_call(
        main_kernel,
        grid=(proj_count // GROUP,),
        in_specs=[
            smem, smem, smem, smem,
            pl.BlockSpec((GROUP, row_count, col_count), lambda g: (g, 0, 0)),
            pl.BlockSpec((row_count, col_count), lambda g: (0, 0), **once),
            pl.BlockSpec((flat_count, row_count, col_count), lambda g: (0, 0, 0), **once),
            pl.BlockSpec((half, half), lambda g: (0, 0), **once),
            pl.BlockSpec((half, half), lambda g: (0, 0), **once),
            pl.BlockSpec((BLK, BLK), lambda g: (0, 0), **once),
            pl.BlockSpec((BLK, BLK), lambda g: (0, 0), **once),
        ],
        out_specs=pl.BlockSpec((3 * row_count, col_count), lambda g: (0, 0)),
        out_shape=jax.ShapeDtypeStruct((3 * row_count, col_count), jnp.float32),
        scratch_shapes=[
            pltpu.VMEM((GROUP * row_count, col_count), jnp.float32),
            pltpu.VMEM((3 * row_count, col_count + 2 * TILE), jnp.bfloat16),
        ],
        compiler_params=pltpu.CompilerParams(
            dimension_semantics=("arbitrary",), vmem_limit_bytes=60 * 1024 * 1024
        ),
    )(flat_weights, stretch, offset, tilt_shift, projections, mean_flat, eigen_flats, ghi, glo, perm, permt)


def per_device(projections, mean_flat, eigen_flats, stretch, offset, tilt_shift):
    proj_count, row_count, col_count = projections.shape
    flat_count = eigen_flats.shape[0]
    total_proj = proj_count * lax.axis_size("angle")
    sampled = eigen_flats[:, ::STRIDE, :]
    targets = (projections[:, ::STRIDE, :] - mean_flat[None, ::STRIDE, :])
    stacked = jnp.concatenate([sampled, targets], axis=0)
    gram_all = jnp.einsum("arc,brc->ab", stacked, stacked, precision=lax.Precision.HIGHEST)
    gram_all = lax.psum(gram_all, "row")
    gram_matrix = gram_all[:flat_count, :flat_count]
    rhs_matrix = gram_all[:flat_count, flat_count:]
    gram_matrix = gram_matrix + col_count * jnp.eye(flat_count, dtype=jnp.float32)
    cholesky_factor = jnp.linalg.cholesky(gram_matrix)
    middle = lax.linalg.triangular_solve(cholesky_factor, rhs_matrix, left_side=True, lower=True)
    solved = lax.linalg.triangular_solve(
        cholesky_factor, middle, left_side=True, lower=True, transpose_a=True
    )
    flat_weights = solved.T
    layer_block = deposit(
        flat_weights, stretch, offset, tilt_shift, projections, mean_flat, eigen_flats
    )
    summed_block = lax.psum_scatter(layer_block, "angle", scatter_dimension=1, tiled=True)
    from_next = shifted(summed_block[row_count : 2 * row_count], "row", 1)
    from_second = shifted(summed_block[2 * row_count :], "row", 2)
    summed = summed_block[:row_count] + from_next + from_second
    return summed / math.sqrt(total_proj)


def solution(mesh):
    return jax.shard_map(
        per_device,
        mesh=mesh,
        in_specs=(
            P("angle", "row", None),
            P("row", None),
            P(None, "row", None),
            P("angle"),
            P("angle"),
            P("angle"),
        ),
        out_specs=P("row", "angle"),
        check_vma=False,
    )
```

```python
import math

import jax
import jax.numpy as jnp
from jax import lax
from jax.experimental import pallas as pl
from jax.experimental.pallas import tpu as pltpu
from jax.sharding import PartitionSpec as P

TILE = 128
STRIDE = 4
GROUP = 4
BLK = 256
CHUNK = 16


def shifted(value, axis, by):
    size = lax.axis_size(axis)
    pairs = [(i, i + by) for i in range(size) if 0 <= i + by < size]
    return lax.ppermute(value, axis, pairs)


def split_bf16(x):
    hi = x.astype(jnp.bfloat16)
    lo = (x - hi.astype(jnp.float32)).astype(jnp.bfloat16)
    return hi, lo


def half_table(half):
    idx = lax.optimization_barrier(jnp.arange(half, dtype=jnp.int32))
    dist = (2 * (idx[None, :] - idx[:, None]) + 1).astype(jnp.float32)
    table = -1.0 / (math.pi * math.pi * dist * dist)
    return split_bf16(table)


def block_perm():
    rows = jnp.arange(BLK, dtype=jnp.int32)[:, None]
    cols = jnp.arange(BLK, dtype=jnp.int32)[None, :]
    target = rows // 2 + (BLK // 2) * (rows % 2)
    perm = (cols == target).astype(jnp.bfloat16)
    return perm, perm.T


def dot(a, b):
    return jnp.dot(a, b, preferred_element_type=jnp.float32)


def dot_nt(a, b):
    return lax.dot_general(a, b, (((1,), (1,)), ((), ())), preferred_element_type=jnp.float32)


def main_kernel(w_ref, st_ref, off_ref, tilt_ref, proj_ref, mean_ref, e_ref, ghi_ref, glo_ref,
                perm_ref, permt_ref, out_ref, a_scr, fs_scr):
    g = pl.program_id(0)
    flat_count, row_count, col_count = e_ref.shape
    rows = GROUP * row_count
    half = col_count // 2
    nblk = col_count // BLK
    hb = BLK // 2
    tile_count = col_count // TILE

    @pl.when(g == 0)
    def _():
        out_ref[...] = jnp.zeros_like(out_ref)

    for q in range(GROUP):
        p = g * GROUP + q
        wk = [w_ref[p, k] for k in range(flat_count)]

        def absorb_chunk(c, carry):
            r0 = pl.multiple_of(c * CHUNK, CHUNK)
            acc = mean_ref[pl.ds(r0, CHUNK), :] - proj_ref[q, pl.ds(r0, CHUNK), :]
            for k in range(flat_count):
                acc = acc + wk[k] * e_ref[k, pl.ds(r0, CHUNK), :]
            a_scr[pl.ds(q * row_count + r0, CHUNK), :] = acc
            return carry

        lax.fori_loop(0, row_count // CHUNK, absorb_chunk, 0)

    perm = perm_ref[...]
    even_hi, even_lo, odd_hi, odd_lo = [], [], [], []
    for b in range(nblk):
        blk = a_scr[:, b * BLK:(b + 1) * BLK]
        hi, lo = split_bf16(blk)
        ph = dot(hi, perm).astype(jnp.bfloat16)
        po = dot(lo, perm).astype(jnp.bfloat16)
        even_hi.append(ph[:, :hb])
        odd_hi.append(ph[:, hb:])
        even_lo.append(po[:, :hb])
        odd_lo.append(po[:, hb:])
    even_hi = jnp.concatenate(even_hi, axis=1)
    even_lo = jnp.concatenate(even_lo, axis=1)
    odd_hi = jnp.concatenate(odd_hi, axis=1)
    odd_lo = jnp.concatenate(odd_lo, axis=1)
    ghi = ghi_ref[...]
    glo = glo_ref[...]
    f_odd = dot(even_hi, ghi) + dot(even_lo, ghi) + dot(even_hi, glo)
    f_odd = f_odd + 0.25 * (odd_hi.astype(jnp.float32) + odd_lo.astype(jnp.float32))
    f_even = dot_nt(odd_hi, ghi) + dot_nt(odd_lo, ghi) + dot_nt(odd_hi, glo)
    f_even = f_even + 0.25 * (even_hi.astype(jnp.float32) + even_lo.astype(jnp.float32))
    fe = f_even.astype(jnp.bfloat16)
    fo = f_odd.astype(jnp.bfloat16)
    permt = permt_ref[...]
    nat = []
    for b in range(nblk):
        pair = jnp.concatenate([fe[:, b * hb:(b + 1) * hb], fo[:, b * hb:(b + 1) * hb]], axis=1)
        nat.append(dot(pair, permt).astype(jnp.bfloat16))
    filtered = jnp.concatenate(nat, axis=1)

    layer_rows = out_ref.shape[0]
    pad_cols = fs_scr.shape[1] - col_count
    fs_scr[:, col_count:] = jnp.zeros((layer_rows, pad_cols), jnp.bfloat16)
    z_iota = lax.broadcasted_iota(jnp.int32, (layer_rows, row_count), 0)
    r_iota = lax.broadcasted_iota(jnp.int32, (layer_rows, row_count), 1)
    w_iota = lax.broadcasted_iota(jnp.int32, (2 * TILE, TILE), 0)
    i_iota = lax.broadcasted_iota(jnp.int32, (1, TILE), 1)
    for q in range(GROUP):
        p = g * GROUP + q
        stretch_one = st_ref[p]
        offset_one = off_ref[p]
        tilt_one = tilt_ref[p]
        shift = (z_iota == r_iota + tilt_one).astype(jnp.bfloat16)
        fs = dot(shift, filtered[q * row_count:(q + 1) * row_count, :])
        fs_scr[:, :col_count] = fs.astype(jnp.bfloat16)
        scaled = i_iota * stretch_one
        rel = scaled // TILE
        frac = (scaled % TILE).astype(jnp.float32) / TILE

        def tile_body(t, carry):
            lo_col = t * stretch_one + offset_one
            blk_id = lo_col // TILE
            target = rel + (lo_col - blk_id * TILE)
            hat = jnp.where(w_iota == target, 1.0 - frac, 0.0) + jnp.where(w_iota == target + 1, frac, 0.0)
            start = pl.multiple_of(blk_id * TILE, TILE)
            window = fs_scr[:, pl.ds(start, 2 * TILE)]
            img = dot(window, hat.astype(jnp.bfloat16))
            c0 = pl.multiple_of(t * TILE, TILE)
            out_ref[:, pl.ds(c0, TILE)] += img
            return carry

        lax.fori_loop(0, tile_count, tile_body, 0)


def deposit(flat_weights, stretch, offset, tilt_shift, projections, mean_flat, eigen_flats):
    proj_count, row_count, col_count = projections.shape
    flat_count = eigen_flats.shape[0]
    half = col_count // 2
    ghi, glo = half_table(half)
    perm, permt = block_perm()
    smem = pl.BlockSpec(memory_space=pltpu.SMEM)
    once = dict(pipeline_mode=pl.Buffered(1))
    return pl.pallas_call(
        main_kernel,
        grid=(proj_count // GROUP,),
        in_specs=[
            smem, smem, smem, smem,
            pl.BlockSpec((GROUP, row_count, col_count), lambda g: (g, 0, 0)),
            pl.BlockSpec((row_count, col_count), lambda g: (0, 0), **once),
            pl.BlockSpec((flat_count, row_count, col_count), lambda g: (0, 0, 0), **once),
            pl.BlockSpec((half, half), lambda g: (0, 0), **once),
            pl.BlockSpec((half, half), lambda g: (0, 0), **once),
            pl.BlockSpec((BLK, BLK), lambda g: (0, 0), **once),
            pl.BlockSpec((BLK, BLK), lambda g: (0, 0), **once),
        ],
        out_specs=pl.BlockSpec((3 * row_count, col_count), lambda g: (0, 0)),
        out_shape=jax.ShapeDtypeStruct((3 * row_count, col_count), jnp.float32),
        scratch_shapes=[
            pltpu.VMEM((GROUP * row_count, col_count), jnp.float32),
            pltpu.VMEM((3 * row_count, col_count + 2 * TILE), jnp.bfloat16),
        ],
        compiler_params=pltpu.CompilerParams(
            dimension_semantics=("arbitrary",), vmem_limit_bytes=60 * 1024 * 1024
        ),
    )(flat_weights, stretch, offset, tilt_shift, projections, mean_flat, eigen_flats, ghi, glo, perm, permt)


def all_sum(value, axis):
    size = lax.axis_size(axis)
    if size & (size - 1):
        total = value
        for by in range(1, size):
            total = total + lax.ppermute(value, axis, [(i, (i + by) % size) for i in range(size)])
        return total
    by = 1
    while by < size:
        value = value + lax.ppermute(value, axis, [(i, i ^ by) for i in range(size)])
        by *= 2
    return value


def gather_kernel(e_ref, p_ref, m_ref, es_ref, ts_ref):
    samples, flat_count, _ = es_ref.shape
    proj_count = ts_ref.shape[1]
    row_count = m_ref.shape[0]
    for s in range(samples):
        r = STRIDE * s
        mean_row = m_ref[pl.ds(r, 1), :]
        for k in range(flat_count):
            es_ref[s, pl.ds(k, 1), :] = e_ref[pl.ds(k * row_count + r, 1), :]
        for p in range(proj_count):
            ts_ref[s, pl.ds(p, 1), :] = p_ref[pl.ds(p * row_count + r, 1), :] - mean_row


def sampled_rows(projections, mean_flat, eigen_flats):
    proj_count, row_count, col_count = projections.shape
    flat_count = eigen_flats.shape[0]
    samples = row_count // STRIDE
    return pl.pallas_call(
        gather_kernel,
        out_shape=(
            jax.ShapeDtypeStruct((samples, flat_count, col_count), jnp.float32),
            jax.ShapeDtypeStruct((samples, proj_count, col_count), jnp.float32),
        ),
        compiler_params=pltpu.CompilerParams(vmem_limit_bytes=60 * 1024 * 1024),
    )(
        eigen_flats.reshape(flat_count * row_count, col_count),
        projections.reshape(proj_count * row_count, col_count),
        mean_flat,
    )


def per_device(projections, mean_flat, eigen_flats, stretch, offset, tilt_shift):
    proj_count, row_count, col_count = projections.shape
    flat_count = eigen_flats.shape[0]
    total_proj = proj_count * lax.axis_size("angle")
    sampled, targets = sampled_rows(projections, mean_flat, eigen_flats)
    gram_part = jnp.einsum("sac,sbc->ab", sampled, sampled, precision=lax.Precision.HIGHEST)
    rhs_part = jnp.einsum("sac,sbc->ab", sampled, targets, precision=lax.Precision.HIGHEST)
    gram_all = all_sum(jnp.concatenate([gram_part, rhs_part], axis=1), "row")
    gram_matrix = gram_all[:, :flat_count]
    rhs_matrix = gram_all[:, flat_count:]
    gram_matrix = gram_matrix + col_count * jnp.eye(flat_count, dtype=jnp.float32)
    cholesky_factor = jnp.linalg.cholesky(gram_matrix)
    middle = lax.linalg.triangular_solve(cholesky_factor, rhs_matrix, left_side=True, lower=True)
    solved = lax.linalg.triangular_solve(
        cholesky_factor, middle, left_side=True, lower=True, transpose_a=True
    )
    flat_weights = solved.T
    layer_block = deposit(
        flat_weights, stretch, offset, tilt_shift, projections, mean_flat, eigen_flats
    )
    summed_block = lax.psum_scatter(layer_block, "angle", scatter_dimension=1, tiled=True)
    from_next = shifted(summed_block[row_count : 2 * row_count], "row", 1)
    from_second = shifted(summed_block[2 * row_count :], "row", 2)
    summed = summed_block[:row_count] + from_next + from_second
    return summed / math.sqrt(total_proj)


def solution(mesh):
    return jax.shard_map(
        per_device,
        mesh=mesh,
        in_specs=(
            P("angle", "row", None),
            P("row", None),
            P(None, "row", None),
            P("angle"),
            P("angle"),
            P("angle"),
        ),
        out_specs=P("row", "angle"),
        check_vma=False,
    )
```

```python
import math

import jax
import jax.numpy as jnp
from jax import lax
from jax.experimental import pallas as pl
from jax.experimental.pallas import tpu as pltpu
from jax.sharding import PartitionSpec as P

TILE = 128
STRIDE = 4
GROUP = 4
BLK = 256
CHUNK = 16


def shifted(value, axis, by):
    size = lax.axis_size(axis)
    pairs = [(i, i + by) for i in range(size) if 0 <= i + by < size]
    return lax.ppermute(value, axis, pairs)


def split_bf16(x):
    hi = x.astype(jnp.bfloat16)
    lo = (x - hi.astype(jnp.float32)).astype(jnp.bfloat16)
    return hi, lo


def half_table(half):
    idx = lax.optimization_barrier(jnp.arange(half, dtype=jnp.int32))
    dist = (2 * (idx[None, :] - idx[:, None]) + 1).astype(jnp.float32)
    table = -1.0 / (math.pi * math.pi * dist * dist)
    return split_bf16(table)


def block_perm():
    rows = jnp.arange(BLK, dtype=jnp.int32)[:, None]
    cols = jnp.arange(BLK, dtype=jnp.int32)[None, :]
    target = rows // 2 + (BLK // 2) * (rows % 2)
    perm = (cols == target).astype(jnp.bfloat16)
    return perm, perm.T


def dot(a, b):
    return jnp.dot(a, b, preferred_element_type=jnp.float32)


def dot_nt(a, b):
    return lax.dot_general(a, b, (((1,), (1,)), ((), ())), preferred_element_type=jnp.float32)


def main_kernel(w_ref, st_ref, off_ref, tilt_ref, proj_ref, mean_ref, e_ref, ghi_ref, glo_ref,
                perm_ref, permt_ref, out_ref, a_scr, fs_scr, acc_scr):
    g = pl.program_id(0)
    flat_count, row_count, col_count = e_ref.shape
    rows = GROUP * row_count
    half = col_count // 2
    nblk = col_count // BLK
    hb = BLK // 2
    tile_count = col_count // TILE

    @pl.when(g == 0)
    def _():
        acc_scr[...] = jnp.zeros_like(acc_scr)

    for q in range(GROUP):
        p = g * GROUP + q
        wk = [w_ref[p, k] for k in range(flat_count)]

        def absorb_chunk(c, carry):
            r0 = pl.multiple_of(c * CHUNK, CHUNK)
            acc = mean_ref[pl.ds(r0, CHUNK), :] - proj_ref[q, pl.ds(r0, CHUNK), :]
            for k in range(flat_count):
                acc = acc + wk[k] * e_ref[k, pl.ds(r0, CHUNK), :]
            a_scr[pl.ds(q * row_count + r0, CHUNK), :] = acc
            return carry

        lax.fori_loop(0, row_count // CHUNK, absorb_chunk, 0)

    perm = perm_ref[...]
    even_hi, even_lo, odd_hi, odd_lo = [], [], [], []
    for b in range(nblk):
        blk = a_scr[:, b * BLK:(b + 1) * BLK]
        hi, lo = split_bf16(blk)
        ph = dot(hi, perm).astype(jnp.bfloat16)
        po = dot(lo, perm).astype(jnp.bfloat16)
        even_hi.append(ph[:, :hb])
        odd_hi.append(ph[:, hb:])
        even_lo.append(po[:, :hb])
        odd_lo.append(po[:, hb:])
    even_hi = jnp.concatenate(even_hi, axis=1)
    even_lo = jnp.concatenate(even_lo, axis=1)
    odd_hi = jnp.concatenate(odd_hi, axis=1)
    odd_lo = jnp.concatenate(odd_lo, axis=1)
    ghi = ghi_ref[...]
    glo = glo_ref[...]
    f_odd = dot(even_hi, ghi) + dot(even_lo, ghi) + dot(even_hi, glo)
    f_odd = f_odd + 0.25 * (odd_hi.astype(jnp.float32) + odd_lo.astype(jnp.float32))
    f_even = dot_nt(odd_hi, ghi) + dot_nt(odd_lo, ghi) + dot_nt(odd_hi, glo)
    f_even = f_even + 0.25 * (even_hi.astype(jnp.float32) + even_lo.astype(jnp.float32))
    fe = f_even.astype(jnp.bfloat16)
    fo = f_odd.astype(jnp.bfloat16)
    permt = permt_ref[...]
    nat = []
    for b in range(nblk):
        pair = jnp.concatenate([fe[:, b * hb:(b + 1) * hb], fo[:, b * hb:(b + 1) * hb]], axis=1)
        nat.append(dot(pair, permt))
    filtered = jnp.concatenate(nat, axis=1)

    pad_cols = fs_scr.shape[1] - col_count
    fs_scr[:, col_count:] = jnp.zeros((row_count, pad_cols), jnp.float32)
    w_iota = lax.broadcasted_iota(jnp.int32, (2 * TILE, TILE), 0)
    i_iota = lax.broadcasted_iota(jnp.int32, (1, TILE), 1)
    span = 3 * TILE
    for q in range(GROUP):
        p = g * GROUP + q
        stretch_one = st_ref[p]
        offset_one = off_ref[p]
        tilt_one = tilt_ref[p]
        fs_scr[:, :col_count] = filtered[q * row_count:(q + 1) * row_count, :]
        scaled = i_iota * stretch_one
        rel = scaled // TILE
        frac = (scaled % TILE).astype(jnp.float32) / TILE
        hat = jnp.where(w_iota == rel, 1.0 - frac, 0.0) + jnp.where(w_iota == rel + 1, frac, 0.0)
        windows = []
        for t in range(tile_count):
            lo_col = t * stretch_one + offset_one
            blk_id = lo_col // TILE
            start = pl.multiple_of(blk_id * TILE, TILE)
            near = fs_scr[:, pl.ds(start, span)]
            moved = pltpu.roll(near, (span - (lo_col - blk_id * TILE)) % span, 1)
            windows.append(moved[:, :2 * TILE].astype(jnp.bfloat16))
        img = dot(jnp.concatenate(windows, axis=0), hat.astype(jnp.bfloat16))
        image = jnp.concatenate(
            [img[t * row_count:(t + 1) * row_count] for t in range(tile_count)], axis=1
        )
        base = pl.multiple_of((tilt_one // 8) * 8, 8)
        padded = jnp.concatenate([image, jnp.zeros((8, col_count), jnp.float32)], axis=0)
        acc_scr[pl.ds(base, row_count + 8), :] += pltpu.roll(padded, tilt_one % 8, 0)

    @pl.when(g == pl.num_programs(0) - 1)
    def _():
        out_ref[...] = acc_scr[:out_ref.shape[0], :]


def deposit(flat_weights, stretch, offset, tilt_shift, projections, mean_flat, eigen_flats):
    proj_count, row_count, col_count = projections.shape
    flat_count = eigen_flats.shape[0]
    half = col_count // 2
    ghi, glo = half_table(half)
    perm, permt = block_perm()
    smem = pl.BlockSpec(memory_space=pltpu.SMEM)
    once = dict(pipeline_mode=pl.Buffered(1))
    return pl.pallas_call(
        main_kernel,
        grid=(proj_count // GROUP,),
        in_specs=[
            smem, smem, smem, smem,
            pl.BlockSpec((GROUP, row_count, col_count), lambda g: (g, 0, 0)),
            pl.BlockSpec((row_count, col_count), lambda g: (0, 0), **once),
            pl.BlockSpec((flat_count, row_count, col_count), lambda g: (0, 0, 0), **once),
            pl.BlockSpec((half, half), lambda g: (0, 0), **once),
            pl.BlockSpec((half, half), lambda g: (0, 0), **once),
            pl.BlockSpec((BLK, BLK), lambda g: (0, 0), **once),
            pl.BlockSpec((BLK, BLK), lambda g: (0, 0), **once),
        ],
        out_specs=pl.BlockSpec((3 * row_count, col_count), lambda g: (0, 0)),
        out_shape=jax.ShapeDtypeStruct((3 * row_count, col_count), jnp.float32),
        scratch_shapes=[
            pltpu.VMEM((GROUP * row_count, col_count), jnp.float32),
            pltpu.VMEM((row_count, col_count + 2 * TILE), jnp.float32),
            pltpu.VMEM((3 * row_count + 8, col_count), jnp.float32),
        ],
        compiler_params=pltpu.CompilerParams(
            dimension_semantics=("arbitrary",), vmem_limit_bytes=60 * 1024 * 1024
        ),
    )(flat_weights, stretch, offset, tilt_shift, projections, mean_flat, eigen_flats, ghi, glo, perm, permt)


def all_sum(value, axis):
    size = lax.axis_size(axis)
    if size & (size - 1):
        total = value
        for by in range(1, size):
            total = total + lax.ppermute(value, axis, [(i, (i + by) % size) for i in range(size)])
        return total
    by = 1
    while by < size:
        value = value + lax.ppermute(value, axis, [(i, i ^ by) for i in range(size)])
        by *= 2
    return value


def gather_kernel(e_ref, p_ref, m_ref, es_ref, ts_ref):
    samples, flat_count, _ = es_ref.shape
    proj_count = ts_ref.shape[1]
    row_count = m_ref.shape[0]
    for s in range(samples):
        r = STRIDE * s
        mean_row = m_ref[pl.ds(r, 1), :]
        for k in range(flat_count):
            es_ref[s, pl.ds(k, 1), :] = e_ref[pl.ds(k * row_count + r, 1), :]
        for p in range(proj_count):
            ts_ref[s, pl.ds(p, 1), :] = p_ref[pl.ds(p * row_count + r, 1), :] - mean_row


def sampled_rows(projections, mean_flat, eigen_flats):
    proj_count, row_count, col_count = projections.shape
    flat_count = eigen_flats.shape[0]
    samples = row_count // STRIDE
    return pl.pallas_call(
        gather_kernel,
        out_shape=(
            jax.ShapeDtypeStruct((samples, flat_count, col_count), jnp.float32),
            jax.ShapeDtypeStruct((samples, proj_count, col_count), jnp.float32),
        ),
        compiler_params=pltpu.CompilerParams(vmem_limit_bytes=60 * 1024 * 1024),
    )(
        eigen_flats.reshape(flat_count * row_count, col_count),
        projections.reshape(proj_count * row_count, col_count),
        mean_flat,
    )


def per_device(projections, mean_flat, eigen_flats, stretch, offset, tilt_shift):
    proj_count, row_count, col_count = projections.shape
    flat_count = eigen_flats.shape[0]
    total_proj = proj_count * lax.axis_size("angle")
    sampled, targets = sampled_rows(projections, mean_flat, eigen_flats)
    gram_part = jnp.einsum("sac,sbc->ab", sampled, sampled, precision=lax.Precision.HIGHEST)
    rhs_part = jnp.einsum("sac,sbc->ab", sampled, targets, precision=lax.Precision.HIGHEST)
    gram_all = all_sum(jnp.concatenate([gram_part, rhs_part], axis=1), "row")
    gram_matrix = gram_all[:, :flat_count]
    rhs_matrix = gram_all[:, flat_count:]
    gram_matrix = gram_matrix + col_count * jnp.eye(flat_count, dtype=jnp.float32)
    cholesky_factor = jnp.linalg.cholesky(gram_matrix)
    middle = lax.linalg.triangular_solve(cholesky_factor, rhs_matrix, left_side=True, lower=True)
    solved = lax.linalg.triangular_solve(
        cholesky_factor, middle, left_side=True, lower=True, transpose_a=True
    )
    flat_weights = solved.T
    layer_block = deposit(
        flat_weights, stretch, offset, tilt_shift, projections, mean_flat, eigen_flats
    )
    summed_block = lax.psum_scatter(layer_block, "angle", scatter_dimension=1, tiled=True)
    from_next = shifted(summed_block[row_count : 2 * row_count], "row", 1)
    from_second = shifted(summed_block[2 * row_count :], "row", 2)
    summed = summed_block[:row_count] + from_next + from_second
    return summed / math.sqrt(total_proj)


def solution(mesh):
    return jax.shard_map(
        per_device,
        mesh=mesh,
        in_specs=(
            P("angle", "row", None),
            P("row", None),
            P(None, "row", None),
            P("angle"),
            P("angle"),
            P("angle"),
        ),
        out_specs=P("row", "angle"),
        check_vma=False,
    )
```

```python
import math

import jax
import jax.numpy as jnp
from jax import lax
from jax.experimental import pallas as pl
from jax.experimental.pallas import tpu as pltpu
from jax.sharding import PartitionSpec as P

TILE = 128
STRIDE = 4
GROUP = 4
BLK = 256
CHUNK = 16


def shifted(value, axis, by):
    size = lax.axis_size(axis)
    pairs = [(i, i + by) for i in range(size) if 0 <= i + by < size]
    return lax.ppermute(value, axis, pairs)


def split_bf16(x):
    hi = x.astype(jnp.bfloat16)
    lo = (x - hi.astype(jnp.float32)).astype(jnp.bfloat16)
    return hi, lo


def half_table(half):
    idx = lax.optimization_barrier(jnp.arange(half, dtype=jnp.int32))
    dist = (2 * (idx[None, :] - idx[:, None]) + 1).astype(jnp.float32)
    table = -1.0 / (math.pi * math.pi * dist * dist)
    return split_bf16(table)


def block_perm():
    rows = jnp.arange(BLK, dtype=jnp.int32)[:, None]
    cols = jnp.arange(BLK, dtype=jnp.int32)[None, :]
    target = rows // 2 + (BLK // 2) * (rows % 2)
    perm = (cols == target).astype(jnp.bfloat16)
    return perm, perm.T


def dot(a, b):
    return jnp.dot(a, b, preferred_element_type=jnp.float32)


def dot_nt(a, b):
    return lax.dot_general(a, b, (((1,), (1,)), ((), ())), preferred_element_type=jnp.float32)


def main_kernel(w_ref, st_ref, off_ref, tilt_ref, proj_ref, mean_ref, e_ref, ghi_ref, glo_ref,
                perm_ref, permt_ref, out_ref, a_scr, fs_scr, acc_scr):
    g = pl.program_id(0)
    flat_count, row_count, col_count = e_ref.shape
    rows = GROUP * row_count
    half = col_count // 2
    nblk = col_count // BLK
    hb = BLK // 2
    tile_count = col_count // TILE

    @pl.when(g == 0)
    def _():
        acc_scr[...] = jnp.zeros_like(acc_scr)

    for q in range(GROUP):
        p = g * GROUP + q
        wk = [w_ref[p, k] for k in range(flat_count)]

        def absorb_chunk(c, carry):
            r0 = pl.multiple_of(c * CHUNK, CHUNK)
            acc = mean_ref[pl.ds(r0, CHUNK), :] - proj_ref[q, pl.ds(r0, CHUNK), :]
            for k in range(flat_count):
                acc = acc + wk[k] * e_ref[k, pl.ds(r0, CHUNK), :]
            a_scr[pl.ds(q * row_count + r0, CHUNK), :] = acc
            return carry

        lax.fori_loop(0, row_count // CHUNK, absorb_chunk, 0)

    perm = perm_ref[...]
    even_hi, even_lo, odd_hi, odd_lo = [], [], [], []
    for b in range(nblk):
        blk = a_scr[:, b * BLK:(b + 1) * BLK]
        hi, lo = split_bf16(blk)
        ph = dot(hi, perm).astype(jnp.bfloat16)
        po = dot(lo, perm).astype(jnp.bfloat16)
        even_hi.append(ph[:, :hb])
        odd_hi.append(ph[:, hb:])
        even_lo.append(po[:, :hb])
        odd_lo.append(po[:, hb:])
    even_hi = jnp.concatenate(even_hi, axis=1)
    even_lo = jnp.concatenate(even_lo, axis=1)
    odd_hi = jnp.concatenate(odd_hi, axis=1)
    odd_lo = jnp.concatenate(odd_lo, axis=1)
    ghi = ghi_ref[...]
    glo = glo_ref[...]
    f_odd = dot(even_hi, ghi) + dot(even_lo, ghi) + dot(even_hi, glo)
    f_odd = f_odd + 0.25 * (odd_hi.astype(jnp.float32) + odd_lo.astype(jnp.float32))
    f_even = dot_nt(odd_hi, ghi) + dot_nt(odd_lo, ghi) + dot_nt(odd_hi, glo)
    f_even = f_even + 0.25 * (even_hi.astype(jnp.float32) + even_lo.astype(jnp.float32))
    fe = f_even.astype(jnp.bfloat16)
    fo = f_odd.astype(jnp.bfloat16)
    permt = permt_ref[...]
    nat = []
    for b in range(nblk):
        pair = jnp.concatenate([fe[:, b * hb:(b + 1) * hb], fo[:, b * hb:(b + 1) * hb]], axis=1)
        nat.append(dot(pair, permt))
    filtered = jnp.concatenate(nat, axis=1)

    pad_cols = fs_scr.shape[1] - col_count
    fs_scr[:, col_count:] = jnp.zeros((row_count, pad_cols), jnp.float32)
    w_iota = lax.broadcasted_iota(jnp.int32, (2 * TILE, TILE), 0)
    i_iota = lax.broadcasted_iota(jnp.int32, (1, TILE), 1)
    span = 3 * TILE
    for q in range(GROUP):
        p = g * GROUP + q
        stretch_one = st_ref[p]
        offset_one = off_ref[p]
        tilt_one = tilt_ref[p]
        fs_scr[:, :col_count] = filtered[q * row_count:(q + 1) * row_count, :]
        scaled = i_iota * stretch_one
        rel = scaled // TILE
        frac = (scaled % TILE).astype(jnp.float32) / TILE
        hat = jnp.where(w_iota == rel, 1.0 - frac, 0.0) + jnp.where(w_iota == rel + 1, frac, 0.0)
        windows = []
        for t in range(tile_count):
            lo_col = t * stretch_one + offset_one
            blk_id = lo_col // TILE
            start = pl.multiple_of(blk_id * TILE, TILE)
            near = fs_scr[:, pl.ds(start, span)]
            moved = pltpu.roll(near, (span - (lo_col - blk_id * TILE)) % span, 1)
            windows.append(moved[:, :2 * TILE].astype(jnp.bfloat16))
        img = dot(jnp.concatenate(windows, axis=0), hat.astype(jnp.bfloat16))
        image = jnp.concatenate(
            [img[t * row_count:(t + 1) * row_count] for t in range(tile_count)], axis=1
        )
        base = pl.multiple_of((tilt_one // 8) * 8, 8)
        padded = jnp.concatenate([image, jnp.zeros((8, col_count), jnp.float32)], axis=0)
        acc_scr[pl.ds(base, row_count + 8), :] += pltpu.roll(padded, tilt_one % 8, 0)

    @pl.when(g == pl.num_programs(0) - 1)
    def _():
        out_ref[...] = acc_scr[:out_ref.shape[0], :]


def deposit(flat_weights, stretch, offset, tilt_shift, projections, mean_flat, eigen_flats):
    proj_count, row_count, col_count = projections.shape
    flat_count = eigen_flats.shape[0]
    half = col_count // 2
    ghi, glo = half_table(half)
    perm, permt = block_perm()
    smem = pl.BlockSpec(memory_space=pltpu.SMEM)
    once = dict(pipeline_mode=pl.Buffered(1))
    return pl.pallas_call(
        main_kernel,
        grid=(proj_count // GROUP,),
        in_specs=[
            smem, smem, smem, smem,
            pl.BlockSpec((GROUP, row_count, col_count), lambda g: (g, 0, 0)),
            pl.BlockSpec((row_count, col_count), lambda g: (0, 0), **once),
            pl.BlockSpec((flat_count, row_count, col_count), lambda g: (0, 0, 0), **once),
            pl.BlockSpec((half, half), lambda g: (0, 0), **once),
            pl.BlockSpec((half, half), lambda g: (0, 0), **once),
            pl.BlockSpec((BLK, BLK), lambda g: (0, 0), **once),
            pl.BlockSpec((BLK, BLK), lambda g: (0, 0), **once),
        ],
        out_specs=pl.BlockSpec((3 * row_count, col_count), lambda g: (0, 0)),
        out_shape=jax.ShapeDtypeStruct((3 * row_count, col_count), jnp.float32),
        scratch_shapes=[
            pltpu.VMEM((GROUP * row_count, col_count), jnp.float32),
            pltpu.VMEM((row_count, col_count + 2 * TILE), jnp.float32),
            pltpu.VMEM((3 * row_count + 8, col_count), jnp.float32),
        ],
        compiler_params=pltpu.CompilerParams(
            dimension_semantics=("arbitrary",), vmem_limit_bytes=60 * 1024 * 1024
        ),
    )(flat_weights, stretch, offset, tilt_shift, projections, mean_flat, eigen_flats, ghi, glo, perm, permt)


def all_sum(value, axis):
    size = lax.axis_size(axis)
    if size & (size - 1):
        total = value
        for by in range(1, size):
            total = total + lax.ppermute(value, axis, [(i, (i + by) % size) for i in range(size)])
        return total
    by = 1
    while by < size:
        value = value + lax.ppermute(value, axis, [(i, i ^ by) for i in range(size)])
        by *= 2
    return value


def gather_kernel(e_ref, p_ref, m_ref, es_ref, ts_ref):
    samples, flat_count, _ = es_ref.shape
    proj_count = ts_ref.shape[1]
    row_count = m_ref.shape[0]
    for s in range(samples):
        r = STRIDE * s
        mean_row = m_ref[pl.ds(r, 1), :]
        for k in range(flat_count):
            es_ref[s, pl.ds(k, 1), :] = e_ref[pl.ds(k * row_count + r, 1), :]
        for p in range(proj_count):
            ts_ref[s, pl.ds(p, 1), :] = p_ref[pl.ds(p * row_count + r, 1), :] - mean_row


def sampled_rows(projections, mean_flat, eigen_flats):
    proj_count, row_count, col_count = projections.shape
    flat_count = eigen_flats.shape[0]
    samples = row_count // STRIDE
    return pl.pallas_call(
        gather_kernel,
        out_shape=(
            jax.ShapeDtypeStruct((samples, flat_count, col_count), jnp.float32),
            jax.ShapeDtypeStruct((samples, proj_count, col_count), jnp.float32),
        ),
        compiler_params=pltpu.CompilerParams(vmem_limit_bytes=60 * 1024 * 1024),
    )(
        eigen_flats.reshape(flat_count * row_count, col_count),
        projections.reshape(proj_count * row_count, col_count),
        mean_flat,
    )


def scatter_sum(block, axis):
    size = lax.axis_size(axis)
    if size & (size - 1):
        return lax.psum_scatter(block, axis, scatter_dimension=1, tiled=True)
    rows, cols = block.shape
    me = lax.axis_index(axis)
    bits = size.bit_length() - 1
    current = block.reshape((rows,) + (2,) * bits + (cols // size,))
    for level in range(bits):
        side = (me >> level) & 1
        dim = current.ndim - 2
        keep = lax.dynamic_index_in_dim(current, side, dim, keepdims=False)
        give = lax.dynamic_index_in_dim(current, 1 - side, dim, keepdims=False)
        got = lax.ppermute(give, axis, [(i, i ^ (1 << level)) for i in range(size)])
        current = keep + got
    return current


def per_device(projections, mean_flat, eigen_flats, stretch, offset, tilt_shift):
    proj_count, row_count, col_count = projections.shape
    flat_count = eigen_flats.shape[0]
    total_proj = proj_count * lax.axis_size("angle")
    sampled, targets = sampled_rows(projections, mean_flat, eigen_flats)
    gram_part = jnp.einsum("sac,sbc->ab", sampled, sampled, precision=lax.Precision.HIGHEST)
    rhs_part = jnp.einsum("sac,sbc->ab", sampled, targets, precision=lax.Precision.HIGHEST)
    gram_all = all_sum(jnp.concatenate([gram_part, rhs_part], axis=1), "row")
    gram_matrix = gram_all[:, :flat_count]
    rhs_matrix = gram_all[:, flat_count:]
    gram_matrix = gram_matrix + col_count * jnp.eye(flat_count, dtype=jnp.float32)
    cholesky_factor = jnp.linalg.cholesky(gram_matrix)
    middle = lax.linalg.triangular_solve(cholesky_factor, rhs_matrix, left_side=True, lower=True)
    solved = lax.linalg.triangular_solve(
        cholesky_factor, middle, left_side=True, lower=True, transpose_a=True
    )
    flat_weights = solved.T
    layer_block = deposit(
        flat_weights, stretch, offset, tilt_shift, projections, mean_flat, eigen_flats
    )
    summed_block = scatter_sum(layer_block, "angle")
    from_next = shifted(summed_block[row_count : 2 * row_count], "row", 1)
    from_second = shifted(summed_block[2 * row_count :], "row", 2)
    summed = summed_block[:row_count] + from_next + from_second
    return summed / math.sqrt(total_proj)


def solution(mesh):
    return jax.shard_map(
        per_device,
        mesh=mesh,
        in_specs=(
            P("angle", "row", None),
            P("row", None),
            P(None, "row", None),
            P("angle"),
            P("angle"),
            P("angle"),
        ),
        out_specs=P("row", "angle"),
        check_vma=False,
    )
```

```python
import math

import jax
import jax.numpy as jnp
from jax import lax
from jax.experimental import pallas as pl
from jax.experimental.pallas import tpu as pltpu
from jax.sharding import PartitionSpec as P

TILE = 128
STRIDE = 4
GROUP = 4
BLK = 256
CHUNK = 16


def shifted(value, axis, by):
    size = lax.axis_size(axis)
    pairs = [(i, i + by) for i in range(size) if 0 <= i + by < size]
    return lax.ppermute(value, axis, pairs)


def split_bf16(x):
    hi = x.astype(jnp.bfloat16)
    lo = (x - hi.astype(jnp.float32)).astype(jnp.bfloat16)
    return hi, lo


def half_table(half):
    idx = lax.optimization_barrier(jnp.arange(half, dtype=jnp.int32))
    dist = (2 * (idx[None, :] - idx[:, None]) + 1).astype(jnp.float32)
    table = -1.0 / (math.pi * math.pi * dist * dist)
    return split_bf16(table)


def block_perm():
    rows = jnp.arange(BLK, dtype=jnp.int32)[:, None]
    cols = jnp.arange(BLK, dtype=jnp.int32)[None, :]
    target = rows // 2 + (BLK // 2) * (rows % 2)
    perm = (cols == target).astype(jnp.bfloat16)
    return perm, perm.T


def dot(a, b):
    return jnp.dot(a, b, preferred_element_type=jnp.float32)


def dot_nt(a, b):
    return lax.dot_general(a, b, (((1,), (1,)), ((), ())), preferred_element_type=jnp.float32)


def main_kernel(w_ref, st_ref, off_ref, tilt_ref, proj_ref, mean_ref, e_ref, ghi_ref, glo_ref,
                perm_ref, permt_ref, out_ref, a_scr, fs_scr, acc_scr):
    g = pl.program_id(0)
    flat_count, row_count, col_count = e_ref.shape
    rows = GROUP * row_count
    half = col_count // 2
    nblk = col_count // BLK
    hb = BLK // 2
    tile_count = col_count // TILE

    @pl.when(g == 0)
    def _():
        acc_scr[...] = jnp.zeros_like(acc_scr)

    for q in range(GROUP):
        p = g * GROUP + q
        wk = [w_ref[p, k] for k in range(flat_count)]

        def absorb_chunk(c, carry):
            r0 = pl.multiple_of(c * CHUNK, CHUNK)
            acc = mean_ref[pl.ds(r0, CHUNK), :] - proj_ref[q, pl.ds(r0, CHUNK), :]
            for k in range(flat_count):
                acc = acc + wk[k] * e_ref[k, pl.ds(r0, CHUNK), :]
            a_scr[pl.ds(q * row_count + r0, CHUNK), :] = acc
            return carry

        lax.fori_loop(0, row_count // CHUNK, absorb_chunk, 0)

    perm = perm_ref[...]
    even_hi, even_lo, odd_hi, odd_lo = [], [], [], []
    for b in range(nblk):
        blk = a_scr[:, b * BLK:(b + 1) * BLK]
        hi, lo = split_bf16(blk)
        ph = dot(hi, perm).astype(jnp.bfloat16)
        po = dot(lo, perm).astype(jnp.bfloat16)
        even_hi.append(ph[:, :hb])
        odd_hi.append(ph[:, hb:])
        even_lo.append(po[:, :hb])
        odd_lo.append(po[:, hb:])
    even_hi = jnp.concatenate(even_hi, axis=1)
    even_lo = jnp.concatenate(even_lo, axis=1)
    odd_hi = jnp.concatenate(odd_hi, axis=1)
    odd_lo = jnp.concatenate(odd_lo, axis=1)
    ghi = ghi_ref[...]
    glo = glo_ref[...]
    f_odd = dot(even_hi, ghi) + dot(even_lo, ghi) + dot(even_hi, glo)
    f_odd = f_odd + 0.25 * (odd_hi.astype(jnp.float32) + odd_lo.astype(jnp.float32))
    f_even = dot_nt(odd_hi, ghi) + dot_nt(odd_lo, ghi) + dot_nt(odd_hi, glo)
    f_even = f_even + 0.25 * (even_hi.astype(jnp.float32) + even_lo.astype(jnp.float32))
    fe = f_even.astype(jnp.bfloat16)
    fo = f_odd.astype(jnp.bfloat16)
    permt = permt_ref[...]
    nat = []
    for b in range(nblk):
        pair = jnp.concatenate([fe[:, b * hb:(b + 1) * hb], fo[:, b * hb:(b + 1) * hb]], axis=1)
        nat.append(dot(pair, permt))
    filtered = jnp.concatenate(nat, axis=1)

    pad_cols = fs_scr.shape[1] - col_count
    fs_scr[:, col_count:] = jnp.zeros((row_count, pad_cols), jnp.float32)
    w_iota = lax.broadcasted_iota(jnp.int32, (2 * TILE, TILE), 0)
    i_iota = lax.broadcasted_iota(jnp.int32, (1, TILE), 1)
    span = 3 * TILE
    for q in range(GROUP):
        p = g * GROUP + q
        stretch_one = st_ref[p]
        offset_one = off_ref[p]
        tilt_one = tilt_ref[p]
        fs_scr[:, :col_count] = filtered[q * row_count:(q + 1) * row_count, :]
        scaled = i_iota * stretch_one
        rel = scaled // TILE
        frac = (scaled % TILE).astype(jnp.float32) / TILE
        hat = jnp.where(w_iota == rel, 1.0 - frac, 0.0) + jnp.where(w_iota == rel + 1, frac, 0.0)
        windows = []
        for t in range(tile_count):
            lo_col = t * stretch_one + offset_one
            blk_id = lo_col // TILE
            start = pl.multiple_of(blk_id * TILE, TILE)
            near = fs_scr[:, pl.ds(start, span)]
            moved = pltpu.roll(near, (span - (lo_col - blk_id * TILE)) % span, 1)
            windows.append(moved[:, :2 * TILE].astype(jnp.bfloat16))
        img = dot(jnp.concatenate(windows, axis=0), hat.astype(jnp.bfloat16))
        image = jnp.concatenate(
            [img[t * row_count:(t + 1) * row_count] for t in range(tile_count)], axis=1
        )
        base = pl.multiple_of((tilt_one // 8) * 8, 8)
        padded = jnp.concatenate([image, jnp.zeros((8, col_count), jnp.float32)], axis=0)
        acc_scr[pl.ds(base, row_count + 8), :] += pltpu.roll(padded, tilt_one % 8, 0)

    @pl.when(g == pl.num_programs(0) - 1)
    def _():
        out_ref[...] = acc_scr[:out_ref.shape[0], :]


def deposit(flat_weights, stretch, offset, tilt_shift, projections, mean_flat, eigen_flats):
    proj_count, row_count, col_count = projections.shape
    flat_count = eigen_flats.shape[0]
    half = col_count // 2
    ghi, glo = half_table(half)
    perm, permt = block_perm()
    smem = pl.BlockSpec(memory_space=pltpu.SMEM)
    once = dict(pipeline_mode=pl.Buffered(1))
    return pl.pallas_call(
        main_kernel,
        grid=(proj_count // GROUP,),
        in_specs=[
            smem, smem, smem, smem,
            pl.BlockSpec((GROUP, row_count, col_count), lambda g: (g, 0, 0)),
            pl.BlockSpec((row_count, col_count), lambda g: (0, 0), **once),
            pl.BlockSpec((flat_count, row_count, col_count), lambda g: (0, 0, 0), **once),
            pl.BlockSpec((half, half), lambda g: (0, 0), **once),
            pl.BlockSpec((half, half), lambda g: (0, 0), **once),
            pl.BlockSpec((BLK, BLK), lambda g: (0, 0), **once),
            pl.BlockSpec((BLK, BLK), lambda g: (0, 0), **once),
        ],
        out_specs=pl.BlockSpec((3 * row_count, col_count), lambda g: (0, 0)),
        out_shape=jax.ShapeDtypeStruct((3 * row_count, col_count), jnp.float32),
        scratch_shapes=[
            pltpu.VMEM((GROUP * row_count, col_count), jnp.float32),
            pltpu.VMEM((row_count, col_count + 2 * TILE), jnp.float32),
            pltpu.VMEM((3 * row_count + 8, col_count), jnp.float32),
        ],
        compiler_params=pltpu.CompilerParams(
            dimension_semantics=("arbitrary",), vmem_limit_bytes=60 * 1024 * 1024
        ),
    )(flat_weights, stretch, offset, tilt_shift, projections, mean_flat, eigen_flats, ghi, glo, perm, permt)


def all_sum(value, axis):
    size = lax.axis_size(axis)
    if size & (size - 1):
        total = value
        for by in range(1, size):
            total = total + lax.ppermute(value, axis, [(i, (i + by) % size) for i in range(size)])
        return total
    by = 1
    while by < size:
        value = value + lax.ppermute(value, axis, [(i, i ^ by) for i in range(size)])
        by *= 2
    return value


def gram_kernel(e_ref, p_ref, m_ref, o_ref, x_scr):
    flat_count, block_rows, _ = e_ref.shape
    proj_count = p_ref.shape[0]

    @pl.when(pl.program_id(0) == 0)
    def _():
        x_scr[...] = jnp.zeros_like(x_scr)
        o_ref[...] = jnp.zeros_like(o_ref)

    acc = o_ref[...]
    for r in range(0, block_rows, STRIDE):
        mean_row = m_ref[pl.ds(r, 1), :]
        for k in range(flat_count):
            x_scr[pl.ds(k, 1), :] = e_ref[k, pl.ds(r, 1), :]
        for p in range(proj_count):
            x_scr[pl.ds(flat_count + p, 1), :] = p_ref[p, pl.ds(r, 1), :] - mean_row
        xs = x_scr[...]
        acc = acc + lax.dot_general(
            xs, xs, (((1,), (1,)), ((), ())),
            precision=lax.Precision.HIGHEST, preferred_element_type=jnp.float32,
        )
    o_ref[...] = acc


def sampled_gram(projections, mean_flat, eigen_flats):
    proj_count, row_count, col_count = projections.shape
    flat_count = eigen_flats.shape[0]
    width = -(-(flat_count + proj_count) // 8) * 8
    block_rows = 8
    return pl.pallas_call(
        gram_kernel,
        grid=(row_count // block_rows,),
        in_specs=[
            pl.BlockSpec((flat_count, block_rows, col_count), lambda i: (0, i, 0)),
            pl.BlockSpec((proj_count, block_rows, col_count), lambda i: (0, i, 0)),
            pl.BlockSpec((block_rows, col_count), lambda i: (i, 0)),
        ],
        out_specs=pl.BlockSpec((width, width), lambda i: (0, 0)),
        out_shape=jax.ShapeDtypeStruct((width, width), jnp.float32),
        scratch_shapes=[pltpu.VMEM((width, col_count), jnp.float32)],
        compiler_params=pltpu.CompilerParams(dimension_semantics=("arbitrary",)),
    )(eigen_flats, projections, mean_flat)


def scatter_sum(block, axis):
    size = lax.axis_size(axis)
    if size & (size - 1):
        return lax.psum_scatter(block, axis, scatter_dimension=1, tiled=True)
    rows, cols = block.shape
    me = lax.axis_index(axis)
    bits = size.bit_length() - 1
    current = block.reshape((rows,) + (2,) * bits + (cols // size,))
    for level in range(bits):
        side = (me >> level) & 1
        dim = current.ndim - 2
        keep = lax.dynamic_index_in_dim(current, side, dim, keepdims=False)
        give = lax.dynamic_index_in_dim(current, 1 - side, dim, keepdims=False)
        got = lax.ppermute(give, axis, [(i, i ^ (1 << level)) for i in range(size)])
        current = keep + got
    return current


def per_device(projections, mean_flat, eigen_flats, stretch, offset, tilt_shift):
    proj_count, row_count, col_count = projections.shape
    flat_count = eigen_flats.shape[0]
    total_proj = proj_count * lax.axis_size("angle")
    gram_part = sampled_gram(projections, mean_flat, eigen_flats)
    gram_all = all_sum(gram_part, "row")
    gram_matrix = gram_all[:flat_count, :flat_count]
    rhs_matrix = gram_all[:flat_count, flat_count:flat_count + proj_count]
    gram_matrix = gram_matrix + col_count * jnp.eye(flat_count, dtype=jnp.float32)
    cholesky_factor = jnp.linalg.cholesky(gram_matrix)
    middle = lax.linalg.triangular_solve(cholesky_factor, rhs_matrix, left_side=True, lower=True)
    solved = lax.linalg.triangular_solve(
        cholesky_factor, middle, left_side=True, lower=True, transpose_a=True
    )
    flat_weights = solved.T
    layer_block = deposit(
        flat_weights, stretch, offset, tilt_shift, projections, mean_flat, eigen_flats
    )
    summed_block = scatter_sum(layer_block, "angle")
    from_next = shifted(summed_block[row_count : 2 * row_count], "row", 1)
    from_second = shifted(summed_block[2 * row_count :], "row", 2)
    summed = summed_block[:row_count] + from_next + from_second
    return summed / math.sqrt(total_proj)


def solution(mesh):
    return jax.shard_map(
        per_device,
        mesh=mesh,
        in_specs=(
            P("angle", "row", None),
            P("row", None),
            P(None, "row", None),
            P("angle"),
            P("angle"),
            P("angle"),
        ),
        out_specs=P("row", "angle"),
        check_vma=False,
    )
```

```python
import math

import jax
import jax.numpy as jnp
from jax import lax
from jax.experimental import pallas as pl
from jax.experimental.pallas import tpu as pltpu
from jax.sharding import PartitionSpec as P

TILE = 128
STRIDE = 4
GROUP = 4
BLK = 256
CHUNK = 16


def shifted(value, axis, by):
    size = lax.axis_size(axis)
    pairs = [(i, i + by) for i in range(size) if 0 <= i + by < size]
    return lax.ppermute(value, axis, pairs)


def split_bf16(x):
    hi = x.astype(jnp.bfloat16)
    lo = (x - hi.astype(jnp.float32)).astype(jnp.bfloat16)
    return hi, lo


def half_table(half):
    idx = lax.optimization_barrier(jnp.arange(half, dtype=jnp.int32))
    dist = (2 * (idx[None, :] - idx[:, None]) + 1).astype(jnp.float32)
    table = -1.0 / (math.pi * math.pi * dist * dist)
    return split_bf16(table)


def block_perm():
    rows = jnp.arange(BLK, dtype=jnp.int32)[:, None]
    cols = jnp.arange(BLK, dtype=jnp.int32)[None, :]
    target = rows // 2 + (BLK // 2) * (rows % 2)
    perm = (cols == target).astype(jnp.bfloat16)
    return perm, perm.T


def dot(a, b):
    return jnp.dot(a, b, preferred_element_type=jnp.float32)


def dot_nt(a, b):
    return lax.dot_general(a, b, (((1,), (1,)), ((), ())), preferred_element_type=jnp.float32)


def main_kernel(w_ref, st_ref, off_ref, tilt_ref, proj_ref, mean_ref, e_ref, ghi_ref, glo_ref,
                perm_ref, permt_ref, me_ref, out_ref, a_scr, fs_scr, acc_scr):
    g = pl.program_id(0)
    flat_count, row_count, col_count = e_ref.shape
    rows = GROUP * row_count
    half = col_count // 2
    nblk = col_count // BLK
    hb = BLK // 2
    tile_count = col_count // TILE

    @pl.when(g == 0)
    def _():
        acc_scr[...] = jnp.zeros_like(acc_scr)

    for q in range(GROUP):
        p = g * GROUP + q
        wk = [w_ref[p, k] for k in range(flat_count)]

        def absorb_chunk(c, carry):
            r0 = pl.multiple_of(c * CHUNK, CHUNK)
            acc = mean_ref[pl.ds(r0, CHUNK), :] - proj_ref[q, pl.ds(r0, CHUNK), :]
            for k in range(flat_count):
                acc = acc + wk[k] * e_ref[k, pl.ds(r0, CHUNK), :]
            a_scr[pl.ds(q * row_count + r0, CHUNK), :] = acc
            return carry

        lax.fori_loop(0, row_count // CHUNK, absorb_chunk, 0)

    perm = perm_ref[...]
    even_hi, even_lo, odd_hi, odd_lo = [], [], [], []
    for b in range(nblk):
        blk = a_scr[:, b * BLK:(b + 1) * BLK]
        hi, lo = split_bf16(blk)
        ph = dot(hi, perm).astype(jnp.bfloat16)
        po = dot(lo, perm).astype(jnp.bfloat16)
        even_hi.append(ph[:, :hb])
        odd_hi.append(ph[:, hb:])
        even_lo.append(po[:, :hb])
        odd_lo.append(po[:, hb:])
    even_hi = jnp.concatenate(even_hi, axis=1)
    even_lo = jnp.concatenate(even_lo, axis=1)
    odd_hi = jnp.concatenate(odd_hi, axis=1)
    odd_lo = jnp.concatenate(odd_lo, axis=1)
    ghi = ghi_ref[...]
    glo = glo_ref[...]
    f_odd = dot(even_hi, ghi) + dot(even_lo, ghi) + dot(even_hi, glo)
    f_odd = f_odd + 0.25 * (odd_hi.astype(jnp.float32) + odd_lo.astype(jnp.float32))
    f_even = dot_nt(odd_hi, ghi) + dot_nt(odd_lo, ghi) + dot_nt(odd_hi, glo)
    f_even = f_even + 0.25 * (even_hi.astype(jnp.float32) + even_lo.astype(jnp.float32))
    fe = f_even.astype(jnp.bfloat16)
    fo = f_odd.astype(jnp.bfloat16)
    permt = permt_ref[...]
    nat = []
    for b in range(nblk):
        pair = jnp.concatenate([fe[:, b * hb:(b + 1) * hb], fo[:, b * hb:(b + 1) * hb]], axis=1)
        nat.append(dot(pair, permt))
    filtered = jnp.concatenate(nat, axis=1)

    pad_cols = fs_scr.shape[1] - col_count
    fs_scr[:, col_count:] = jnp.zeros((row_count, pad_cols), jnp.float32)
    w_iota = lax.broadcasted_iota(jnp.int32, (2 * TILE, TILE), 0)
    i_iota = lax.broadcasted_iota(jnp.int32, (1, TILE), 1)
    span = 3 * TILE
    for q in range(GROUP):
        p = g * GROUP + q
        stretch_one = st_ref[p]
        offset_one = off_ref[p]
        tilt_one = tilt_ref[p]
        fs_scr[:, :col_count] = filtered[q * row_count:(q + 1) * row_count, :]
        scaled = i_iota * stretch_one
        rel = scaled // TILE
        frac = (scaled % TILE).astype(jnp.float32) / TILE
        hat = jnp.where(w_iota == rel, 1.0 - frac, 0.0) + jnp.where(w_iota == rel + 1, frac, 0.0)
        windows = []
        for t in range(tile_count):
            lo_col = t * stretch_one + offset_one
            blk_id = lo_col // TILE
            start = pl.multiple_of(blk_id * TILE, TILE)
            near = fs_scr[:, pl.ds(start, span)]
            moved = pltpu.roll(near, (span - (lo_col - blk_id * TILE)) % span, 1)
            windows.append(moved[:, :2 * TILE].astype(jnp.bfloat16))
        img = dot(jnp.concatenate(windows, axis=0), hat.astype(jnp.bfloat16))
        image = jnp.concatenate(
            [img[t * row_count:(t + 1) * row_count] for t in range(tile_count)], axis=1
        )
        base = pl.multiple_of((tilt_one // 8) * 8, 8)
        padded = jnp.concatenate([image, jnp.zeros((8, col_count), jnp.float32)], axis=0)
        acc_scr[pl.ds(base, row_count + 8), :] += pltpu.roll(padded, tilt_one % 8, 0)

    @pl.when(g == pl.num_programs(0) - 1)
    def _():
        parts, layer_rows, width = out_ref.shape
        me = me_ref[0]
        for pos in range(parts):
            c0 = pl.multiple_of((me ^ pos) * width, TILE)
            out_ref[pos] = acc_scr[:layer_rows, pl.ds(c0, width)]


def deposit(flat_weights, stretch, offset, tilt_shift, projections, mean_flat, eigen_flats, parts, me):
    proj_count, row_count, col_count = projections.shape
    flat_count = eigen_flats.shape[0]
    half = col_count // 2
    ghi, glo = half_table(half)
    perm, permt = block_perm()
    smem = pl.BlockSpec(memory_space=pltpu.SMEM)
    once = dict(pipeline_mode=pl.Buffered(1))
    return pl.pallas_call(
        main_kernel,
        grid=(proj_count // GROUP,),
        in_specs=[
            smem, smem, smem, smem,
            pl.BlockSpec((GROUP, row_count, col_count), lambda g: (g, 0, 0)),
            pl.BlockSpec((row_count, col_count), lambda g: (0, 0), **once),
            pl.BlockSpec((flat_count, row_count, col_count), lambda g: (0, 0, 0), **once),
            pl.BlockSpec((half, half), lambda g: (0, 0), **once),
            pl.BlockSpec((half, half), lambda g: (0, 0), **once),
            pl.BlockSpec((BLK, BLK), lambda g: (0, 0), **once),
            pl.BlockSpec((BLK, BLK), lambda g: (0, 0), **once),
            smem,
        ],
        out_specs=pl.BlockSpec((parts, 3 * row_count, col_count // parts), lambda g: (0, 0, 0)),
        out_shape=jax.ShapeDtypeStruct((parts, 3 * row_count, col_count // parts), jnp.float32),
        scratch_shapes=[
            pltpu.VMEM((GROUP * row_count, col_count), jnp.float32),
            pltpu.VMEM((row_count, col_count + 2 * TILE), jnp.float32),
            pltpu.VMEM((3 * row_count + 8, col_count), jnp.float32),
        ],
        compiler_params=pltpu.CompilerParams(
            dimension_semantics=("arbitrary",), vmem_limit_bytes=60 * 1024 * 1024
        ),
    )(flat_weights, stretch, offset, tilt_shift, projections, mean_flat, eigen_flats, ghi, glo, perm, permt, me)


def all_sum(value, axis):
    size = lax.axis_size(axis)
    if size & (size - 1):
        total = value
        for by in range(1, size):
            total = total + lax.ppermute(value, axis, [(i, (i + by) % size) for i in range(size)])
        return total
    by = 1
    while by < size:
        value = value + lax.ppermute(value, axis, [(i, i ^ by) for i in range(size)])
        by *= 2
    return value


def gram_kernel(e_ref, p_ref, m_ref, o_ref, x_scr):
    flat_count, block_rows, _ = e_ref.shape
    proj_count = p_ref.shape[0]

    @pl.when(pl.program_id(0) == 0)
    def _():
        x_scr[...] = jnp.zeros_like(x_scr)
        o_ref[...] = jnp.zeros_like(o_ref)

    acc = o_ref[...]
    for r in range(0, block_rows, STRIDE):
        mean_row = m_ref[pl.ds(r, 1), :]
        for k in range(flat_count):
            x_scr[pl.ds(k, 1), :] = e_ref[k, pl.ds(r, 1), :]
        for p in range(proj_count):
            x_scr[pl.ds(flat_count + p, 1), :] = p_ref[p, pl.ds(r, 1), :] - mean_row
        xs = x_scr[...]
        acc = acc + lax.dot_general(
            xs, xs, (((1,), (1,)), ((), ())),
            precision=lax.Precision.HIGHEST, preferred_element_type=jnp.float32,
        )
    o_ref[...] = acc


def sampled_gram(projections, mean_flat, eigen_flats):
    proj_count, row_count, col_count = projections.shape
    flat_count = eigen_flats.shape[0]
    width = -(-(flat_count + proj_count) // 8) * 8
    block_rows = 8
    return pl.pallas_call(
        gram_kernel,
        grid=(row_count // block_rows,),
        in_specs=[
            pl.BlockSpec((flat_count, block_rows, col_count), lambda i: (0, i, 0)),
            pl.BlockSpec((proj_count, block_rows, col_count), lambda i: (0, i, 0)),
            pl.BlockSpec((block_rows, col_count), lambda i: (i, 0)),
        ],
        out_specs=pl.BlockSpec((width, width), lambda i: (0, 0)),
        out_shape=jax.ShapeDtypeStruct((width, width), jnp.float32),
        scratch_shapes=[pltpu.VMEM((width, col_count), jnp.float32)],
        compiler_params=pltpu.CompilerParams(dimension_semantics=("arbitrary",)),
    )(eigen_flats, projections, mean_flat)


def scatter_sum(chunks, axis):
    size, rows, width = chunks.shape
    current = chunks
    level = 0
    while current.shape[0] > 1:
        pairs = current.reshape(current.shape[0] // 2, 2, rows, width)
        got = lax.ppermute(pairs[:, 1], axis, [(i, i ^ (1 << level)) for i in range(size)])
        current = pairs[:, 0] + got
        level += 1
    return current[0]


def per_device(projections, mean_flat, eigen_flats, stretch, offset, tilt_shift):
    proj_count, row_count, col_count = projections.shape
    flat_count = eigen_flats.shape[0]
    total_proj = proj_count * lax.axis_size("angle")
    gram_part = sampled_gram(projections, mean_flat, eigen_flats)
    gram_all = all_sum(gram_part, "row")
    gram_matrix = gram_all[:flat_count, :flat_count]
    rhs_matrix = gram_all[:flat_count, flat_count:flat_count + proj_count]
    gram_matrix = gram_matrix + col_count * jnp.eye(flat_count, dtype=jnp.float32)
    cholesky_factor = jnp.linalg.cholesky(gram_matrix)
    middle = lax.linalg.triangular_solve(cholesky_factor, rhs_matrix, left_side=True, lower=True)
    solved = lax.linalg.triangular_solve(
        cholesky_factor, middle, left_side=True, lower=True, transpose_a=True
    )
    flat_weights = solved.T
    angle_count = lax.axis_size("angle")
    if angle_count & (angle_count - 1):
        layer_block = deposit(
            flat_weights, stretch, offset, tilt_shift, projections, mean_flat, eigen_flats,
            1, jnp.zeros((1,), jnp.int32),
        )[0]
        summed_block = lax.psum_scatter(layer_block, "angle", scatter_dimension=1, tiled=True)
    else:
        me = lax.axis_index("angle").astype(jnp.int32).reshape(1)
        chunks = deposit(
            flat_weights, stretch, offset, tilt_shift, projections, mean_flat, eigen_flats,
            angle_count, me,
        )
        summed_block = scatter_sum(chunks, "angle")
    from_next = shifted(summed_block[row_count : 2 * row_count], "row", 1)
    from_second = shifted(summed_block[2 * row_count :], "row", 2)
    summed = summed_block[:row_count] + from_next + from_second
    return summed / math.sqrt(total_proj)


def solution(mesh):
    return jax.shard_map(
        per_device,
        mesh=mesh,
        in_specs=(
            P("angle", "row", None),
            P("row", None),
            P(None, "row", None),
            P("angle"),
            P("angle"),
            P("angle"),
        ),
        out_specs=P("row", "angle"),
        check_vma=False,
    )
```

```python
import math

import jax
import jax.numpy as jnp
from jax import lax
from jax.experimental import pallas as pl
from jax.experimental.pallas import tpu as pltpu
from jax.sharding import PartitionSpec as P

TILE = 128
STRIDE = 4
GROUP = 4
BLK = 256
CHUNK = 16


def shifted(value, axis, by):
    size = lax.axis_size(axis)
    pairs = [(i, i + by) for i in range(size) if 0 <= i + by < size]
    return lax.ppermute(value, axis, pairs)


def split_bf16(x):
    hi = x.astype(jnp.bfloat16)
    lo = (x - hi.astype(jnp.float32)).astype(jnp.bfloat16)
    return hi, lo


def half_table(half):
    idx = lax.optimization_barrier(jnp.arange(half, dtype=jnp.int32))
    dist = (2 * (idx[None, :] - idx[:, None]) + 1).astype(jnp.float32)
    table = -1.0 / (math.pi * math.pi * dist * dist)
    return split_bf16(table)


def block_perm():
    rows = jnp.arange(BLK, dtype=jnp.int32)[:, None]
    cols = jnp.arange(BLK, dtype=jnp.int32)[None, :]
    target = rows // 2 + (BLK // 2) * (rows % 2)
    perm = (cols == target).astype(jnp.bfloat16)
    return perm, perm.T


def dot(a, b):
    return jnp.dot(a, b, preferred_element_type=jnp.float32)


def dot_nt(a, b):
    return lax.dot_general(a, b, (((1,), (1,)), ((), ())), preferred_element_type=jnp.float32)


def main_kernel(w_ref, st_ref, off_ref, tilt_ref, proj_ref, mean_ref, e_ref, ghi_ref, glo_ref,
                perm_ref, permt_ref, me_ref, own_ref, out_ref, a_scr, fs_scr, acc_scr):
    g = pl.program_id(0)
    flat_count, row_count, col_count = e_ref.shape
    rows = GROUP * row_count
    half = col_count // 2
    nblk = col_count // BLK
    hb = BLK // 2
    tile_count = col_count // TILE

    @pl.when(g == 0)
    def _():
        acc_scr[...] = jnp.zeros_like(acc_scr)

    for q in range(GROUP):
        p = g * GROUP + q
        wk = [w_ref[p, k] for k in range(flat_count)]

        def absorb_chunk(c, carry):
            r0 = pl.multiple_of(c * CHUNK, CHUNK)
            acc = mean_ref[pl.ds(r0, CHUNK), :] - proj_ref[q, pl.ds(r0, CHUNK), :]
            for k in range(flat_count):
                acc = acc + wk[k] * e_ref[k, pl.ds(r0, CHUNK), :]
            a_scr[pl.ds(q * row_count + r0, CHUNK), :] = acc
            return carry

        lax.fori_loop(0, row_count // CHUNK, absorb_chunk, 0)

    perm = perm_ref[...]
    even_hi, even_lo, odd_hi, odd_lo = [], [], [], []
    for b in range(nblk):
        blk = a_scr[:, b * BLK:(b + 1) * BLK]
        hi, lo = split_bf16(blk)
        ph = dot(hi, perm).astype(jnp.bfloat16)
        po = dot(lo, perm).astype(jnp.bfloat16)
        even_hi.append(ph[:, :hb])
        odd_hi.append(ph[:, hb:])
        even_lo.append(po[:, :hb])
        odd_lo.append(po[:, hb:])
    even_hi = jnp.concatenate(even_hi, axis=1)
    even_lo = jnp.concatenate(even_lo, axis=1)
    odd_hi = jnp.concatenate(odd_hi, axis=1)
    odd_lo = jnp.concatenate(odd_lo, axis=1)
    ghi = ghi_ref[...]
    glo = glo_ref[...]
    f_odd = dot(even_hi, ghi) + dot(even_lo, ghi) + dot(even_hi, glo)
    f_odd = f_odd + 0.25 * (odd_hi.astype(jnp.float32) + odd_lo.astype(jnp.float32))
    f_even = dot_nt(odd_hi, ghi) + dot_nt(odd_lo, ghi) + dot_nt(odd_hi, glo)
    f_even = f_even + 0.25 * (even_hi.astype(jnp.float32) + even_lo.astype(jnp.float32))
    fe = f_even.astype(jnp.bfloat16)
    fo = f_odd.astype(jnp.bfloat16)
    permt = permt_ref[...]
    nat = []
    for b in range(nblk):
        pair = jnp.concatenate([fe[:, b * hb:(b + 1) * hb], fo[:, b * hb:(b + 1) * hb]], axis=1)
        nat.append(dot(pair, permt))
    filtered = jnp.concatenate(nat, axis=1)

    pad_cols = fs_scr.shape[1] - col_count
    fs_scr[:, col_count:] = jnp.zeros((row_count, pad_cols), jnp.float32)
    w_iota = lax.broadcasted_iota(jnp.int32, (2 * TILE, TILE), 0)
    i_iota = lax.broadcasted_iota(jnp.int32, (1, TILE), 1)
    span = 3 * TILE
    for q in range(GROUP):
        p = g * GROUP + q
        stretch_one = st_ref[p]
        offset_one = off_ref[p]
        tilt_one = tilt_ref[p]
        fs_scr[:, :col_count] = filtered[q * row_count:(q + 1) * row_count, :]
        scaled = i_iota * stretch_one
        rel = scaled // TILE
        frac = (scaled % TILE).astype(jnp.float32) / TILE
        hat = jnp.where(w_iota == rel, 1.0 - frac, 0.0) + jnp.where(w_iota == rel + 1, frac, 0.0)
        windows = []
        for t in range(tile_count):
            lo_col = t * stretch_one + offset_one
            blk_id = lo_col // TILE
            start = pl.multiple_of(blk_id * TILE, TILE)
            near = fs_scr[:, pl.ds(start, span)]
            moved = pltpu.roll(near, (span - (lo_col - blk_id * TILE)) % span, 1)
            windows.append(moved[:, :2 * TILE].astype(jnp.bfloat16))
        img = dot(jnp.concatenate(windows, axis=0), hat.astype(jnp.bfloat16))
        image = jnp.concatenate(
            [img[t * row_count:(t + 1) * row_count] for t in range(tile_count)], axis=1
        )
        base = pl.multiple_of((tilt_one // 8) * 8, 8)
        padded = jnp.concatenate([image, jnp.zeros((8, col_count), jnp.float32)], axis=0)
        acc_scr[pl.ds(base, row_count + 8), :] += pltpu.roll(padded, tilt_one % 8, 0)

    @pl.when(g == pl.num_programs(0) - 1)
    def _():
        parts, own_rows, width = own_ref.shape
        layer_rows = own_rows + out_ref.shape[1]
        me = me_ref[0]
        for pos in range(parts):
            c0 = pl.multiple_of((me ^ pos) * width, TILE)
            own_ref[pos] = acc_scr[:own_rows, pl.ds(c0, width)]
            out_ref[pos] = acc_scr[own_rows:layer_rows, pl.ds(c0, width)]


def deposit(flat_weights, stretch, offset, tilt_shift, projections, mean_flat, eigen_flats, parts, me):
    proj_count, row_count, col_count = projections.shape
    flat_count = eigen_flats.shape[0]
    half = col_count // 2
    ghi, glo = half_table(half)
    perm, permt = block_perm()
    smem = pl.BlockSpec(memory_space=pltpu.SMEM)
    once = dict(pipeline_mode=pl.Buffered(1))
    return pl.pallas_call(
        main_kernel,
        grid=(proj_count // GROUP,),
        in_specs=[
            smem, smem, smem, smem,
            pl.BlockSpec((GROUP, row_count, col_count), lambda g: (g, 0, 0)),
            pl.BlockSpec((row_count, col_count), lambda g: (0, 0), **once),
            pl.BlockSpec((flat_count, row_count, col_count), lambda g: (0, 0, 0), **once),
            pl.BlockSpec((half, half), lambda g: (0, 0), **once),
            pl.BlockSpec((half, half), lambda g: (0, 0), **once),
            pl.BlockSpec((BLK, BLK), lambda g: (0, 0), **once),
            pl.BlockSpec((BLK, BLK), lambda g: (0, 0), **once),
            smem,
        ],
        out_specs=[
            pl.BlockSpec((parts, row_count, col_count // parts), lambda g: (0, 0, 0)),
            pl.BlockSpec((parts, 2 * row_count, col_count // parts), lambda g: (0, 0, 0)),
        ],
        out_shape=[
            jax.ShapeDtypeStruct((parts, row_count, col_count // parts), jnp.float32),
            jax.ShapeDtypeStruct((parts, 2 * row_count, col_count // parts), jnp.float32),
        ],
        scratch_shapes=[
            pltpu.VMEM((GROUP * row_count, col_count), jnp.float32),
            pltpu.VMEM((row_count, col_count + 2 * TILE), jnp.float32),
            pltpu.VMEM((3 * row_count + 8, col_count), jnp.float32),
        ],
        compiler_params=pltpu.CompilerParams(
            dimension_semantics=("arbitrary",), vmem_limit_bytes=60 * 1024 * 1024
        ),
    )(flat_weights, stretch, offset, tilt_shift, projections, mean_flat, eigen_flats, ghi, glo, perm, permt, me)


def all_sum(value, axis):
    size = lax.axis_size(axis)
    if size & (size - 1):
        total = value
        for by in range(1, size):
            total = total + lax.ppermute(value, axis, [(i, (i + by) % size) for i in range(size)])
        return total
    by = 1
    while by < size:
        value = value + lax.ppermute(value, axis, [(i, i ^ by) for i in range(size)])
        by *= 2
    return value


def gram_kernel(e_ref, p_ref, m_ref, o_ref, x_scr):
    flat_count, block_rows, _ = e_ref.shape
    proj_count = p_ref.shape[0]

    @pl.when(pl.program_id(0) == 0)
    def _():
        x_scr[...] = jnp.zeros_like(x_scr)
        o_ref[...] = jnp.zeros_like(o_ref)

    acc = o_ref[...]
    for r in range(0, block_rows, STRIDE):
        mean_row = m_ref[pl.ds(r, 1), :]
        for k in range(flat_count):
            x_scr[pl.ds(k, 1), :] = e_ref[k, pl.ds(r, 1), :]
        for p in range(proj_count):
            x_scr[pl.ds(flat_count + p, 1), :] = p_ref[p, pl.ds(r, 1), :] - mean_row
        xs = x_scr[...]
        acc = acc + lax.dot_general(
            xs, xs, (((1,), (1,)), ((), ())),
            precision=lax.Precision.HIGHEST, preferred_element_type=jnp.float32,
        )
    o_ref[...] = acc


def sampled_gram(projections, mean_flat, eigen_flats):
    proj_count, row_count, col_count = projections.shape
    flat_count = eigen_flats.shape[0]
    width = -(-(flat_count + proj_count) // 8) * 8
    block_rows = 8
    return pl.pallas_call(
        gram_kernel,
        grid=(row_count // block_rows,),
        in_specs=[
            pl.BlockSpec((flat_count, block_rows, col_count), lambda i: (0, i, 0)),
            pl.BlockSpec((proj_count, block_rows, col_count), lambda i: (0, i, 0)),
            pl.BlockSpec((block_rows, col_count), lambda i: (i, 0)),
        ],
        out_specs=pl.BlockSpec((width, width), lambda i: (0, 0)),
        out_shape=jax.ShapeDtypeStruct((width, width), jnp.float32),
        scratch_shapes=[pltpu.VMEM((width, col_count), jnp.float32)],
        compiler_params=pltpu.CompilerParams(dimension_semantics=("arbitrary",)),
    )(eigen_flats, projections, mean_flat)


def scatter_sum(chunks, axis):
    size, rows, width = chunks.shape
    current = chunks
    level = 0
    while current.shape[0] > 1:
        pairs = current.reshape(current.shape[0] // 2, 2, rows, width)
        got = lax.ppermute(pairs[:, 1], axis, [(i, i ^ (1 << level)) for i in range(size)])
        current = pairs[:, 0] + got
        level += 1
    return current[0]


def per_device(projections, mean_flat, eigen_flats, stretch, offset, tilt_shift):
    proj_count, row_count, col_count = projections.shape
    flat_count = eigen_flats.shape[0]
    total_proj = proj_count * lax.axis_size("angle")
    gram_part = sampled_gram(projections, mean_flat, eigen_flats)
    gram_all = all_sum(gram_part, "row")
    gram_matrix = gram_all[:flat_count, :flat_count]
    rhs_matrix = gram_all[:flat_count, flat_count:flat_count + proj_count]
    gram_matrix = gram_matrix + col_count * jnp.eye(flat_count, dtype=jnp.float32)
    cholesky_factor = jnp.linalg.cholesky(gram_matrix)
    middle = lax.linalg.triangular_solve(cholesky_factor, rhs_matrix, left_side=True, lower=True)
    solved = lax.linalg.triangular_solve(
        cholesky_factor, middle, left_side=True, lower=True, transpose_a=True
    )
    flat_weights = solved.T
    angle_count = lax.axis_size("angle")
    if angle_count & (angle_count - 1):
        own, moving = deposit(
            flat_weights, stretch, offset, tilt_shift, projections, mean_flat, eigen_flats,
            1, jnp.zeros((1,), jnp.int32),
        )
        own = lax.psum_scatter(own[0], "angle", scatter_dimension=1, tiled=True)
        moving = lax.psum_scatter(moving[0], "angle", scatter_dimension=1, tiled=True)
    else:
        me = lax.axis_index("angle").astype(jnp.int32).reshape(1)
        own, moving = deposit(
            flat_weights, stretch, offset, tilt_shift, projections, mean_flat, eigen_flats,
            angle_count, me,
        )
        moving = scatter_sum(moving, "angle")
        own = scatter_sum(own, "angle")
    from_next = shifted(moving[:row_count], "row", 1)
    from_second = shifted(moving[row_count:], "row", 2)
    summed = own + from_next + from_second
    return summed / math.sqrt(total_proj)


def solution(mesh):
    return jax.shard_map(
        per_device,
        mesh=mesh,
        in_specs=(
            P("angle", "row", None),
            P("row", None),
            P(None, "row", None),
            P("angle"),
            P("angle"),
            P("angle"),
        ),
        out_specs=P("row", "angle"),
        check_vma=False,
    )
```

```python
import functools
import math

import jax
import jax.numpy as jnp
from jax import lax
from jax.experimental import pallas as pl
from jax.experimental.pallas import tpu as pltpu
from jax.sharding import PartitionSpec as P

TILE = 128
STRIDE = 4
GROUP = 4
BLK = 256
CHUNK = 16


def shifted(value, axis, by):
    size = lax.axis_size(axis)
    pairs = [(i, i + by) for i in range(size) if 0 <= i + by < size]
    return lax.ppermute(value, axis, pairs)


def split_bf16(x):
    hi = x.astype(jnp.bfloat16)
    lo = (x - hi.astype(jnp.float32)).astype(jnp.bfloat16)
    return hi, lo


def half_table(half):
    idx = lax.optimization_barrier(jnp.arange(half, dtype=jnp.int32))
    dist = (2 * (idx[None, :] - idx[:, None]) + 1).astype(jnp.float32)
    table = -1.0 / (math.pi * math.pi * dist * dist)
    return split_bf16(table)


def block_perm():
    rows = jnp.arange(BLK, dtype=jnp.int32)[:, None]
    cols = jnp.arange(BLK, dtype=jnp.int32)[None, :]
    target = rows // 2 + (BLK // 2) * (rows % 2)
    perm = (cols == target).astype(jnp.bfloat16)
    return perm, perm.T


def dot(a, b):
    return jnp.dot(a, b, preferred_element_type=jnp.float32)


def dot_nt(a, b):
    return lax.dot_general(a, b, (((1,), (1,)), ((), ())), preferred_element_type=jnp.float32)


def main_kernel(w_ref, st_ref, off_ref, tilt_ref, proj_ref, mean_ref, e_ref, ghi_ref, glo_ref,
                perm_ref, permt_ref, me_ref, own_ref, out_ref, a_scr, fs_scr, acc_scr):
    g = pl.program_id(0)
    flat_count, row_count, col_count = e_ref.shape
    rows = GROUP * row_count
    half = col_count // 2
    nblk = col_count // BLK
    hb = BLK // 2
    tile_count = col_count // TILE

    @pl.when(g == 0)
    def _():
        acc_scr[...] = jnp.zeros_like(acc_scr)

    for q in range(GROUP):
        p = g * GROUP + q
        wk = [w_ref[p, k] for k in range(flat_count)]

        def absorb_chunk(c, carry):
            r0 = pl.multiple_of(c * CHUNK, CHUNK)
            acc = mean_ref[pl.ds(r0, CHUNK), :] - proj_ref[q, pl.ds(r0, CHUNK), :]
            for k in range(flat_count):
                acc = acc + wk[k] * e_ref[k, pl.ds(r0, CHUNK), :]
            a_scr[pl.ds(q * row_count + r0, CHUNK), :] = acc
            return carry

        lax.fori_loop(0, row_count // CHUNK, absorb_chunk, 0)

    perm = perm_ref[...]
    even_hi, even_lo, odd_hi, odd_lo = [], [], [], []
    for b in range(nblk):
        blk = a_scr[:, b * BLK:(b + 1) * BLK]
        hi, lo = split_bf16(blk)
        ph = dot(hi, perm).astype(jnp.bfloat16)
        po = dot(lo, perm).astype(jnp.bfloat16)
        even_hi.append(ph[:, :hb])
        odd_hi.append(ph[:, hb:])
        even_lo.append(po[:, :hb])
        odd_lo.append(po[:, hb:])
    even_hi = jnp.concatenate(even_hi, axis=1)
    even_lo = jnp.concatenate(even_lo, axis=1)
    odd_hi = jnp.concatenate(odd_hi, axis=1)
    odd_lo = jnp.concatenate(odd_lo, axis=1)
    ghi = ghi_ref[...]
    glo = glo_ref[...]
    f_odd = dot(even_hi, ghi) + dot(even_lo, ghi) + dot(even_hi, glo)
    f_odd = f_odd + 0.25 * (odd_hi.astype(jnp.float32) + odd_lo.astype(jnp.float32))
    f_even = dot_nt(odd_hi, ghi) + dot_nt(odd_lo, ghi) + dot_nt(odd_hi, glo)
    f_even = f_even + 0.25 * (even_hi.astype(jnp.float32) + even_lo.astype(jnp.float32))
    fe = f_even.astype(jnp.bfloat16)
    fo = f_odd.astype(jnp.bfloat16)
    permt = permt_ref[...]
    nat = []
    for b in range(nblk):
        pair = jnp.concatenate([fe[:, b * hb:(b + 1) * hb], fo[:, b * hb:(b + 1) * hb]], axis=1)
        nat.append(dot(pair, permt))
    filtered = jnp.concatenate(nat, axis=1)

    pad_cols = fs_scr.shape[1] - col_count
    fs_scr[:, col_count:] = jnp.zeros((row_count, pad_cols), jnp.float32)
    w_iota = lax.broadcasted_iota(jnp.int32, (2 * TILE, TILE), 0)
    i_iota = lax.broadcasted_iota(jnp.int32, (1, TILE), 1)
    span = 3 * TILE
    for q in range(GROUP):
        p = g * GROUP + q
        stretch_one = st_ref[p]
        offset_one = off_ref[p]
        tilt_one = tilt_ref[p]
        fs_scr[:, :col_count] = filtered[q * row_count:(q + 1) * row_count, :]
        scaled = i_iota * stretch_one
        rel = scaled // TILE
        frac = (scaled % TILE).astype(jnp.float32) / TILE
        hat = jnp.where(w_iota == rel, 1.0 - frac, 0.0) + jnp.where(w_iota == rel + 1, frac, 0.0)
        windows = []
        for t in range(tile_count):
            lo_col = t * stretch_one + offset_one
            blk_id = lo_col // TILE
            start = pl.multiple_of(blk_id * TILE, TILE)
            near = fs_scr[:, pl.ds(start, span)]
            moved = pltpu.roll(near, (span - (lo_col - blk_id * TILE)) % span, 1)
            windows.append(moved[:, :2 * TILE].astype(jnp.bfloat16))
        img = dot(jnp.concatenate(windows, axis=0), hat.astype(jnp.bfloat16))
        image = jnp.concatenate(
            [img[t * row_count:(t + 1) * row_count] for t in range(tile_count)], axis=1
        )
        base = pl.multiple_of((tilt_one // 8) * 8, 8)
        padded = jnp.concatenate([image, jnp.zeros((8, col_count), jnp.float32)], axis=0)
        acc_scr[pl.ds(base, row_count + 8), :] += pltpu.roll(padded, tilt_one % 8, 0)

    @pl.when(g == pl.num_programs(0) - 1)
    def _():
        parts, own_rows, width = own_ref.shape
        layer_rows = own_rows + out_ref.shape[1]
        me = me_ref[0]
        for pos in range(parts):
            c0 = pl.multiple_of((me ^ pos) * width, TILE)
            own_ref[pos] = acc_scr[:own_rows, pl.ds(c0, width)]
            out_ref[pos] = acc_scr[own_rows:layer_rows, pl.ds(c0, width)]


def deposit(flat_weights, stretch, offset, tilt_shift, projections, mean_flat, eigen_flats, parts, me):
    proj_count, row_count, col_count = projections.shape
    flat_count = eigen_flats.shape[0]
    half = col_count // 2
    ghi, glo = half_table(half)
    perm, permt = block_perm()
    smem = pl.BlockSpec(memory_space=pltpu.SMEM)
    once = dict(pipeline_mode=pl.Buffered(1))
    return pl.pallas_call(
        main_kernel,
        grid=(proj_count // GROUP,),
        in_specs=[
            smem, smem, smem, smem,
            pl.BlockSpec((GROUP, row_count, col_count), lambda g: (g, 0, 0)),
            pl.BlockSpec((row_count, col_count), lambda g: (0, 0), **once),
            pl.BlockSpec((flat_count, row_count, col_count), lambda g: (0, 0, 0), **once),
            pl.BlockSpec((half, half), lambda g: (0, 0), **once),
            pl.BlockSpec((half, half), lambda g: (0, 0), **once),
            pl.BlockSpec((BLK, BLK), lambda g: (0, 0), **once),
            pl.BlockSpec((BLK, BLK), lambda g: (0, 0), **once),
            smem,
        ],
        out_specs=[
            pl.BlockSpec((parts, row_count, col_count // parts), lambda g: (0, 0, 0)),
            pl.BlockSpec((parts, 2 * row_count, col_count // parts), lambda g: (0, 0, 0)),
        ],
        out_shape=[
            jax.ShapeDtypeStruct((parts, row_count, col_count // parts), jnp.float32),
            jax.ShapeDtypeStruct((parts, 2 * row_count, col_count // parts), jnp.float32),
        ],
        scratch_shapes=[
            pltpu.VMEM((GROUP * row_count, col_count), jnp.float32),
            pltpu.VMEM((row_count, col_count + 2 * TILE), jnp.float32),
            pltpu.VMEM((3 * row_count + 8, col_count), jnp.float32),
        ],
        compiler_params=pltpu.CompilerParams(
            dimension_semantics=("arbitrary",), vmem_limit_bytes=60 * 1024 * 1024
        ),
    )(flat_weights, stretch, offset, tilt_shift, projections, mean_flat, eigen_flats, ghi, glo, perm, permt, me)


def all_sum(value, axis):
    size = lax.axis_size(axis)
    if size & (size - 1):
        total = value
        for by in range(1, size):
            total = total + lax.ppermute(value, axis, [(i, (i + by) % size) for i in range(size)])
        return total
    by = 1
    while by < size:
        value = value + lax.ppermute(value, axis, [(i, i ^ by) for i in range(size)])
        by *= 2
    return value


def gram_kernel(e_ref, p_ref, m_ref, o_ref, x_scr):
    flat_count, block_rows, _ = e_ref.shape
    proj_count = p_ref.shape[0]

    @pl.when(pl.program_id(0) == 0)
    def _():
        x_scr[...] = jnp.zeros_like(x_scr)
        o_ref[...] = jnp.zeros_like(o_ref)

    acc = o_ref[...]
    for r in range(0, block_rows, STRIDE):
        mean_row = m_ref[pl.ds(r, 1), :]
        for k in range(flat_count):
            x_scr[pl.ds(k, 1), :] = e_ref[k, pl.ds(r, 1), :]
        for p in range(proj_count):
            x_scr[pl.ds(flat_count + p, 1), :] = p_ref[p, pl.ds(r, 1), :] - mean_row
        xs = x_scr[...]
        acc = acc + lax.dot_general(
            xs, xs, (((1,), (1,)), ((), ())),
            precision=lax.Precision.HIGHEST, preferred_element_type=jnp.float32,
        )
    o_ref[...] = acc


def sampled_gram(projections, mean_flat, eigen_flats):
    proj_count, row_count, col_count = projections.shape
    flat_count = eigen_flats.shape[0]
    width = -(-(flat_count + proj_count) // 8) * 8
    block_rows = 8
    return pl.pallas_call(
        gram_kernel,
        grid=(row_count // block_rows,),
        in_specs=[
            pl.BlockSpec((flat_count, block_rows, col_count), lambda i: (0, i, 0)),
            pl.BlockSpec((proj_count, block_rows, col_count), lambda i: (0, i, 0)),
            pl.BlockSpec((block_rows, col_count), lambda i: (i, 0)),
        ],
        out_specs=pl.BlockSpec((width, width), lambda i: (0, 0)),
        out_shape=jax.ShapeDtypeStruct((width, width), jnp.float32),
        scratch_shapes=[pltpu.VMEM((width, col_count), jnp.float32)],
        compiler_params=pltpu.CompilerParams(dimension_semantics=("arbitrary",)),
    )(eigen_flats, projections, mean_flat)


def scatter_sum(chunks, axis):
    size, rows, width = chunks.shape
    current = chunks
    level = 0
    while current.shape[0] > 1:
        pairs = current.reshape(current.shape[0] // 2, 2, rows, width)
        got = lax.ppermute(pairs[:, 1], axis, [(i, i ^ (1 << level)) for i in range(size)])
        current = pairs[:, 0] + got
        level += 1
    return current[0]


def solve_kernel(g_ref, o_ref, *, flat_count, diagonal):
    width = g_ref.shape[0]
    full = g_ref[...]
    row_i = lax.broadcasted_iota(jnp.int32, (width, width), 0)
    col_i = lax.broadcasted_iota(jnp.int32, (width, width), 1)
    rows1 = lax.broadcasted_iota(jnp.int32, (width, 1), 0)
    cols1 = lax.broadcasted_iota(jnp.int32, (1, width), 1)
    inside = (row_i < flat_count) & (col_i < flat_count)
    work = jnp.where(inside, full, 0.0) + jnp.where(inside & (row_i == col_i), diagonal, 0.0)
    rhs = jnp.where((col_i >= flat_count) & (row_i < flat_count), full, 0.0)
    lower = jnp.zeros((width, width), jnp.float32)
    upper = jnp.zeros((width, width), jnp.float32)
    for j in range(flat_count):
        col = jnp.sum(jnp.where(col_i == j, work, 0.0), axis=1, keepdims=True)
        row = jnp.sum(jnp.where(row_i == j, work, 0.0), axis=0, keepdims=True)
        pivot = jnp.sqrt(jnp.sum(jnp.where(rows1 == j, col, 0.0), axis=0, keepdims=True))
        col = jnp.where(rows1 >= j, col / pivot, 0.0)
        row = jnp.where(cols1 >= j, row / pivot, 0.0)
        lower = lower + jnp.where(col_i == j, col, 0.0)
        upper = upper + jnp.where(row_i == j, row, 0.0)
        work = work - col * row
    for j in range(flat_count):
        col = jnp.sum(jnp.where(col_i == j, lower, 0.0), axis=1, keepdims=True)
        diag = jnp.sum(jnp.where(rows1 == j, col, 0.0), axis=0, keepdims=True)
        value = jnp.sum(jnp.where(row_i == j, rhs, 0.0), axis=0, keepdims=True) / diag
        rhs = jnp.where(row_i == j, value, jnp.where(row_i > j, rhs - col * value, rhs))
    for j in reversed(range(flat_count)):
        col = jnp.sum(jnp.where(col_i == j, upper, 0.0), axis=1, keepdims=True)
        diag = jnp.sum(jnp.where(rows1 == j, col, 0.0), axis=0, keepdims=True)
        value = jnp.sum(jnp.where(row_i == j, rhs, 0.0), axis=0, keepdims=True) / diag
        rhs = jnp.where(row_i == j, value, jnp.where(row_i < j, rhs - col * value, rhs))
    o_ref[...] = rhs


def flat_solve(gram_all, flat_count, proj_count, diagonal):
    width = gram_all.shape[0]
    solved = pl.pallas_call(
        functools.partial(solve_kernel, flat_count=flat_count, diagonal=float(diagonal)),
        out_shape=jax.ShapeDtypeStruct((width, width), jnp.float32),
    )(gram_all)
    return solved[:flat_count, flat_count:flat_count + proj_count].T


def per_device(projections, mean_flat, eigen_flats, stretch, offset, tilt_shift):
    proj_count, row_count, col_count = projections.shape
    flat_count = eigen_flats.shape[0]
    total_proj = proj_count * lax.axis_size("angle")
    gram_part = sampled_gram(projections, mean_flat, eigen_flats)
    gram_all = all_sum(gram_part, "row")
    flat_weights = flat_solve(gram_all, flat_count, proj_count, col_count)
    angle_count = lax.axis_size("angle")
    if angle_count & (angle_count - 1):
        own, moving = deposit(
            flat_weights, stretch, offset, tilt_shift, projections, mean_flat, eigen_flats,
            1, jnp.zeros((1,), jnp.int32),
        )
        own = lax.psum_scatter(own[0], "angle", scatter_dimension=1, tiled=True)
        moving = lax.psum_scatter(moving[0], "angle", scatter_dimension=1, tiled=True)
    else:
        me = lax.axis_index("angle").astype(jnp.int32).reshape(1)
        own, moving = deposit(
            flat_weights, stretch, offset, tilt_shift, projections, mean_flat, eigen_flats,
            angle_count, me,
        )
        moving = scatter_sum(moving, "angle")
        own = scatter_sum(own, "angle")
    from_next = shifted(moving[:row_count], "row", 1)
    from_second = shifted(moving[row_count:], "row", 2)
    summed = own + from_next + from_second
    return summed / math.sqrt(total_proj)


def solution(mesh):
    return jax.shard_map(
        per_device,
        mesh=mesh,
        in_specs=(
            P("angle", "row", None),
            P("row", None),
            P(None, "row", None),
            P("angle"),
            P("angle"),
            P("angle"),
        ),
        out_specs=P("row", "angle"),
        check_vma=False,
    )
```

```python
import math

import jax
import jax.numpy as jnp
from jax import lax
from jax.experimental import pallas as pl
from jax.experimental.pallas import tpu as pltpu
from jax.sharding import PartitionSpec as P

TILE = 128
STRIDE = 4
GROUP = 4
BLK = 256
CHUNK = 16


def shifted(value, axis, by):
    size = lax.axis_size(axis)
    pairs = [(i, i + by) for i in range(size) if 0 <= i + by < size]
    return lax.ppermute(value, axis, pairs)


def split_bf16(x):
    hi = x.astype(jnp.bfloat16)
    lo = (x - hi.astype(jnp.float32)).astype(jnp.bfloat16)
    return hi, lo


def half_table(half):
    idx = lax.optimization_barrier(jnp.arange(half, dtype=jnp.int32))
    dist = (2 * (idx[None, :] - idx[:, None]) + 1).astype(jnp.float32)
    table = -1.0 / (math.pi * math.pi * dist * dist)
    return split_bf16(table)


def block_perm():
    rows = jnp.arange(BLK, dtype=jnp.int32)[:, None]
    cols = jnp.arange(BLK, dtype=jnp.int32)[None, :]
    target = rows // 2 + (BLK // 2) * (rows % 2)
    perm = (cols == target).astype(jnp.bfloat16)
    return perm, perm.T


def dot(a, b):
    return jnp.dot(a, b, preferred_element_type=jnp.float32)


def dot_nt(a, b):
    return lax.dot_general(a, b, (((1,), (1,)), ((), ())), preferred_element_type=jnp.float32)


def main_kernel(w_ref, st_ref, off_ref, tilt_ref, proj_ref, mean_ref, e_hbm, ghi_hbm, glo_hbm,
                perm_ref, permt_ref, me_ref, own_ref, out_ref, a_scr, fs_scr, acc_scr,
                e_ref, ghi_ref, glo_ref, sem):
    g = pl.program_id(0)
    flat_count, row_count, col_count = e_ref.shape
    chunks = row_count // CHUNK

    def slab_copy(c, k):
        rows_c = pl.ds(pl.multiple_of(c * CHUNK, CHUNK), CHUNK)
        return pltpu.make_async_copy(e_hbm.at[k, rows_c, :], e_ref.at[k, rows_c, :], sem.at[c, k])

    table_copies = [
        pltpu.make_async_copy(ghi_hbm, ghi_ref, sem.at[chunks, 0]),
        pltpu.make_async_copy(glo_hbm, glo_ref, sem.at[chunks, 1]),
    ]

    @pl.when(g == 0)
    def _():
        for c in range(chunks):
            for k in range(flat_count):
                slab_copy(c, k).start()
        for copy in table_copies:
            copy.start()
    rows = GROUP * row_count
    half = col_count // 2
    nblk = col_count // BLK
    hb = BLK // 2
    tile_count = col_count // TILE

    @pl.when(g == 0)
    def _():
        acc_scr[...] = jnp.zeros_like(acc_scr)

    weights = [[w_ref[g * GROUP + q, k] for k in range(flat_count)] for q in range(GROUP)]

    def absorb_chunk(c, carry):
        @pl.when(g == 0)
        def _():
            for k in range(flat_count):
                slab_copy(c, k).wait()

        r0 = pl.multiple_of(c * CHUNK, CHUNK)
        mean_rows = mean_ref[pl.ds(r0, CHUNK), :]
        for q in range(GROUP):
            acc = mean_rows - proj_ref[q, pl.ds(r0, CHUNK), :]
            for k in range(flat_count):
                acc = acc + weights[q][k] * e_ref[k, pl.ds(r0, CHUNK), :]
            a_scr[pl.ds(q * row_count + r0, CHUNK), :] = acc
        return carry

    lax.fori_loop(0, chunks, absorb_chunk, 0)

    @pl.when(g == 0)
    def _():
        for copy in table_copies:
            copy.wait()

    perm = perm_ref[...]
    even_hi, even_lo, odd_hi, odd_lo = [], [], [], []
    for b in range(nblk):
        blk = a_scr[:, b * BLK:(b + 1) * BLK]
        hi, lo = split_bf16(blk)
        ph = dot(hi, perm).astype(jnp.bfloat16)
        po = dot(lo, perm).astype(jnp.bfloat16)
        even_hi.append(ph[:, :hb])
        odd_hi.append(ph[:, hb:])
        even_lo.append(po[:, :hb])
        odd_lo.append(po[:, hb:])
    even_hi = jnp.concatenate(even_hi, axis=1)
    even_lo = jnp.concatenate(even_lo, axis=1)
    odd_hi = jnp.concatenate(odd_hi, axis=1)
    odd_lo = jnp.concatenate(odd_lo, axis=1)
    ghi = ghi_ref[...]
    glo = glo_ref[...]
    f_odd = dot(even_hi, ghi) + dot(even_lo, ghi) + dot(even_hi, glo)
    f_odd = f_odd + 0.25 * (odd_hi.astype(jnp.float32) + odd_lo.astype(jnp.float32))
    f_even = dot_nt(odd_hi, ghi) + dot_nt(odd_lo, ghi) + dot_nt(odd_hi, glo)
    f_even = f_even + 0.25 * (even_hi.astype(jnp.float32) + even_lo.astype(jnp.float32))
    fe = f_even.astype(jnp.bfloat16)
    fo = f_odd.astype(jnp.bfloat16)
    permt = permt_ref[...]
    nat = []
    for b in range(nblk):
        pair = jnp.concatenate([fe[:, b * hb:(b + 1) * hb], fo[:, b * hb:(b + 1) * hb]], axis=1)
        nat.append(dot(pair, permt))
    filtered = jnp.concatenate(nat, axis=1)

    pad_cols = fs_scr.shape[1] - col_count
    fs_scr[:, col_count:] = jnp.zeros((row_count, pad_cols), jnp.float32)
    w_iota = lax.broadcasted_iota(jnp.int32, (2 * TILE, TILE), 0)
    i_iota = lax.broadcasted_iota(jnp.int32, (1, TILE), 1)
    span = 3 * TILE
    for q in range(GROUP):
        p = g * GROUP + q
        stretch_one = st_ref[p]
        offset_one = off_ref[p]
        tilt_one = tilt_ref[p]
        fs_scr[:, :col_count] = filtered[q * row_count:(q + 1) * row_count, :]
        scaled = i_iota * stretch_one
        rel = scaled // TILE
        frac = (scaled % TILE).astype(jnp.float32) / TILE
        hat = jnp.where(w_iota == rel, 1.0 - frac, 0.0) + jnp.where(w_iota == rel + 1, frac, 0.0)
        windows = []
        for t in range(tile_count):
            lo_col = t * stretch_one + offset_one
            blk_id = lo_col // TILE
            start = pl.multiple_of(blk_id * TILE, TILE)
            near = fs_scr[:, pl.ds(start, span)]
            moved = pltpu.roll(near, (span - (lo_col - blk_id * TILE)) % span, 1)
            windows.append(moved[:, :2 * TILE].astype(jnp.bfloat16))
        img = dot(jnp.concatenate(windows, axis=0), hat.astype(jnp.bfloat16))
        image = jnp.concatenate(
            [img[t * row_count:(t + 1) * row_count] for t in range(tile_count)], axis=1
        )
        base = pl.multiple_of((tilt_one // 8) * 8, 8)
        padded = jnp.concatenate([image, jnp.zeros((8, col_count), jnp.float32)], axis=0)
        acc_scr[pl.ds(base, row_count + 8), :] += pltpu.roll(padded, tilt_one % 8, 0)

    @pl.when(g == pl.num_programs(0) - 1)
    def _():
        parts, own_rows, width = own_ref.shape
        layer_rows = own_rows + out_ref.shape[1]
        me = me_ref[0]
        for pos in range(parts):
            c0 = pl.multiple_of((me ^ pos) * width, TILE)
            own_ref[pos] = acc_scr[:own_rows, pl.ds(c0, width)]
            out_ref[pos] = acc_scr[own_rows:layer_rows, pl.ds(c0, width)]


def deposit(flat_weights, stretch, offset, tilt_shift, projections, mean_flat, eigen_flats, parts, me):
    proj_count, row_count, col_count = projections.shape
    flat_count = eigen_flats.shape[0]
    half = col_count // 2
    ghi, glo = half_table(half)
    perm, permt = block_perm()
    smem = pl.BlockSpec(memory_space=pltpu.SMEM)
    once = dict(pipeline_mode=pl.Buffered(1))
    return pl.pallas_call(
        main_kernel,
        grid=(proj_count // GROUP,),
        in_specs=[
            smem, smem, smem, smem,
            pl.BlockSpec((GROUP, row_count, col_count), lambda g: (g, 0, 0)),
            pl.BlockSpec((row_count, col_count), lambda g: (0, 0), **once),
            pl.BlockSpec(memory_space=pl.ANY),
            pl.BlockSpec(memory_space=pl.ANY),
            pl.BlockSpec(memory_space=pl.ANY),
            pl.BlockSpec((BLK, BLK), lambda g: (0, 0), **once),
            pl.BlockSpec((BLK, BLK), lambda g: (0, 0), **once),
            smem,
        ],
        out_specs=[
            pl.BlockSpec((parts, row_count, col_count // parts), lambda g: (0, 0, 0)),
            pl.BlockSpec((parts, 2 * row_count, col_count // parts), lambda g: (0, 0, 0)),
        ],
        out_shape=[
            jax.ShapeDtypeStruct((parts, row_count, col_count // parts), jnp.float32),
            jax.ShapeDtypeStruct((parts, 2 * row_count, col_count // parts), jnp.float32),
        ],
        scratch_shapes=[
            pltpu.VMEM((GROUP * row_count, col_count), jnp.float32),
            pltpu.VMEM((row_count, col_count + 2 * TILE), jnp.float32),
            pltpu.VMEM((3 * row_count + 8, col_count), jnp.float32),
            pltpu.VMEM((flat_count, row_count, col_count), jnp.float32),
            pltpu.VMEM((half, half), jnp.bfloat16),
            pltpu.VMEM((half, half), jnp.bfloat16),
            pltpu.SemaphoreType.DMA((row_count // CHUNK + 1, max(flat_count, 2))),
        ],
        compiler_params=pltpu.CompilerParams(
            dimension_semantics=("arbitrary",), vmem_limit_bytes=60 * 1024 * 1024
        ),
    )(flat_weights, stretch, offset, tilt_shift, projections, mean_flat, eigen_flats, ghi, glo, perm, permt, me)


def all_sum(value, axis):
    size = lax.axis_size(axis)
    if size & (size - 1):
        total = value
        for by in range(1, size):
            total = total + lax.ppermute(value, axis, [(i, (i + by) % size) for i in range(size)])
        return total
    by = 1
    while by < size:
        value = value + lax.ppermute(value, axis, [(i, i ^ by) for i in range(size)])
        by *= 2
    return value


def gram_kernel(e_ref, p_ref, m_ref, o_ref, x_scr):
    flat_count, block_rows, _ = e_ref.shape
    proj_count = p_ref.shape[0]

    @pl.when(pl.program_id(0) == 0)
    def _():
        x_scr[...] = jnp.zeros_like(x_scr)
        o_ref[...] = jnp.zeros_like(o_ref)

    acc = o_ref[...]
    for r in range(0, block_rows, STRIDE):
        mean_row = m_ref[pl.ds(r, 1), :]
        for k in range(flat_count):
            x_scr[pl.ds(k, 1), :] = e_ref[k, pl.ds(r, 1), :]
        for p in range(proj_count):
            x_scr[pl.ds(flat_count + p, 1), :] = p_ref[p, pl.ds(r, 1), :] - mean_row
        xs = x_scr[...]
        acc = acc + lax.dot_general(
            xs, xs, (((1,), (1,)), ((), ())),
            precision=lax.Precision.HIGHEST, preferred_element_type=jnp.float32,
        )
    o_ref[...] = acc


def sampled_gram(projections, mean_flat, eigen_flats):
    proj_count, row_count, col_count = projections.shape
    flat_count = eigen_flats.shape[0]
    width = -(-(flat_count + proj_count) // 8) * 8
    block_rows = 8
    return pl.pallas_call(
        gram_kernel,
        grid=(row_count // block_rows,),
        in_specs=[
            pl.BlockSpec((flat_count, block_rows, col_count), lambda i: (0, i, 0)),
            pl.BlockSpec((proj_count, block_rows, col_count), lambda i: (0, i, 0)),
            pl.BlockSpec((block_rows, col_count), lambda i: (i, 0)),
        ],
        out_specs=pl.BlockSpec((width, width), lambda i: (0, 0)),
        out_shape=jax.ShapeDtypeStruct((width, width), jnp.float32),
        scratch_shapes=[pltpu.VMEM((width, col_count), jnp.float32)],
        compiler_params=pltpu.CompilerParams(dimension_semantics=("arbitrary",)),
    )(eigen_flats, projections, mean_flat)


def scatter_sum(chunks, axis):
    size, rows, width = chunks.shape
    current = chunks
    level = 0
    while current.shape[0] > 1:
        pairs = current.reshape(current.shape[0] // 2, 2, rows, width)
        got = lax.ppermute(pairs[:, 1], axis, [(i, i ^ (1 << level)) for i in range(size)])
        current = pairs[:, 0] + got
        level += 1
    return current[0]


def per_device(projections, mean_flat, eigen_flats, stretch, offset, tilt_shift):
    proj_count, row_count, col_count = projections.shape
    flat_count = eigen_flats.shape[0]
    total_proj = proj_count * lax.axis_size("angle")
    gram_part = sampled_gram(projections, mean_flat, eigen_flats)
    gram_all = all_sum(gram_part, "row")
    gram_matrix = gram_all[:flat_count, :flat_count]
    rhs_matrix = gram_all[:flat_count, flat_count:flat_count + proj_count]
    gram_matrix = gram_matrix + col_count * jnp.eye(flat_count, dtype=jnp.float32)
    cholesky_factor = jnp.linalg.cholesky(gram_matrix)
    middle = lax.linalg.triangular_solve(cholesky_factor, rhs_matrix, left_side=True, lower=True)
    solved = lax.linalg.triangular_solve(
        cholesky_factor, middle, left_side=True, lower=True, transpose_a=True
    )
    flat_weights = solved.T
    angle_count = lax.axis_size("angle")
    if angle_count & (angle_count - 1):
        own, moving = deposit(
            flat_weights, stretch, offset, tilt_shift, projections, mean_flat, eigen_flats,
            1, jnp.zeros((1,), jnp.int32),
        )
        own = lax.psum_scatter(own[0], "angle", scatter_dimension=1, tiled=True)
        moving = lax.psum_scatter(moving[0], "angle", scatter_dimension=1, tiled=True)
    else:
        me = lax.axis_index("angle").astype(jnp.int32).reshape(1)
        own, moving = deposit(
            flat_weights, stretch, offset, tilt_shift, projections, mean_flat, eigen_flats,
            angle_count, me,
        )
        moving = scatter_sum(moving, "angle")
        own = scatter_sum(own, "angle")
    from_next = shifted(moving[:row_count], "row", 1)
    from_second = shifted(moving[row_count:], "row", 2)
    summed = own + from_next + from_second
    return summed / math.sqrt(total_proj)


def solution(mesh):
    return jax.shard_map(
        per_device,
        mesh=mesh,
        in_specs=(
            P("angle", "row", None),
            P("row", None),
            P(None, "row", None),
            P("angle"),
            P("angle"),
            P("angle"),
        ),
        out_specs=P("row", "angle"),
        check_vma=False,
    )
```

```python
import math

import jax
import jax.numpy as jnp
from jax import lax
from jax.experimental import pallas as pl
from jax.experimental.pallas import tpu as pltpu
from jax.sharding import PartitionSpec as P

TILE = 128
STRIDE = 4
GROUP = 4
BLK = 256
CHUNK = 16


def shifted(value, axis, by):
    size = lax.axis_size(axis)
    pairs = [(i, i + by) for i in range(size) if 0 <= i + by < size]
    return lax.ppermute(value, axis, pairs)


def split_bf16(x):
    hi = x.astype(jnp.bfloat16)
    lo = (x - hi.astype(jnp.float32)).astype(jnp.bfloat16)
    return hi, lo


def half_table(half):
    idx = lax.optimization_barrier(jnp.arange(half, dtype=jnp.int32))
    dist = (2 * (idx[None, :] - idx[:, None]) + 1).astype(jnp.float32)
    table = -1.0 / (math.pi * math.pi * dist * dist)
    return split_bf16(table)


def block_perm():
    rows = jnp.arange(BLK, dtype=jnp.int32)[:, None]
    cols = jnp.arange(BLK, dtype=jnp.int32)[None, :]
    target = rows // 2 + (BLK // 2) * (rows % 2)
    perm = (cols == target).astype(jnp.bfloat16)
    return perm, perm.T


def dot(a, b):
    return jnp.dot(a, b, preferred_element_type=jnp.float32)


def dot_nt(a, b):
    return lax.dot_general(a, b, (((1,), (1,)), ((), ())), preferred_element_type=jnp.float32)


def main_kernel(w_ref, st_ref, off_ref, tilt_ref, proj_ref, mean_ref, e_hbm, ghi_hbm, glo_hbm,
                perm_ref, permt_ref, me_ref, own_ref, out_ref, a_scr, fs_scr, acc_scr,
                e_ref, ghi_ref, glo_ref, sem):
    g = pl.program_id(0)
    flat_count, row_count, col_count = e_ref.shape
    chunks = row_count // CHUNK

    def slab_copy(c, k):
        rows_c = pl.ds(pl.multiple_of(c * CHUNK, CHUNK), CHUNK)
        return pltpu.make_async_copy(e_hbm.at[k, rows_c, :], e_ref.at[k, rows_c, :], sem.at[c, k])

    table_copies = [
        pltpu.make_async_copy(ghi_hbm, ghi_ref, sem.at[chunks, 0]),
        pltpu.make_async_copy(glo_hbm, glo_ref, sem.at[chunks, 1]),
    ]

    @pl.when(g == 0)
    def _():
        for c in range(chunks):
            for k in range(flat_count):
                slab_copy(c, k).start()
        for copy in table_copies:
            copy.start()
    rows = GROUP * row_count
    half = col_count // 2
    nblk = col_count // BLK
    hb = BLK // 2
    tile_count = col_count // TILE

    @pl.when(g == 0)
    def _():
        acc_scr[...] = jnp.zeros_like(acc_scr)

    weights = [[w_ref[g * GROUP + q, k] for k in range(flat_count)] for q in range(GROUP)]

    def absorb_chunk(c, carry):
        @pl.when(g == 0)
        def _():
            for k in range(flat_count):
                slab_copy(c, k).wait()

        r0 = pl.multiple_of(c * CHUNK, CHUNK)
        mean_rows = mean_ref[pl.ds(r0, CHUNK), :]
        for q in range(GROUP):
            acc = mean_rows - proj_ref[q, pl.ds(r0, CHUNK), :]
            for k in range(flat_count):
                acc = acc + weights[q][k] * e_ref[k, pl.ds(r0, CHUNK), :]
            a_scr[pl.ds(q * row_count + r0, CHUNK), :] = acc
        return carry

    lax.fori_loop(0, chunks, absorb_chunk, 0)

    @pl.when(g == 0)
    def _():
        for copy in table_copies:
            copy.wait()

    perm = perm_ref[...]
    even_hi, even_lo, odd_hi, odd_lo = [], [], [], []
    for b in range(nblk):
        blk = a_scr[:, b * BLK:(b + 1) * BLK]
        hi, lo = split_bf16(blk)
        ph = dot(hi, perm).astype(jnp.bfloat16)
        po = dot(lo, perm).astype(jnp.bfloat16)
        even_hi.append(ph[:, :hb])
        odd_hi.append(ph[:, hb:])
        even_lo.append(po[:, :hb])
        odd_lo.append(po[:, hb:])
    even_hi = jnp.concatenate(even_hi, axis=1)
    even_lo = jnp.concatenate(even_lo, axis=1)
    odd_hi = jnp.concatenate(odd_hi, axis=1)
    odd_lo = jnp.concatenate(odd_lo, axis=1)
    ghi = ghi_ref[...]
    glo = glo_ref[...]
    f_odd = dot(even_hi, ghi) + dot(even_lo, ghi) + dot(even_hi, glo)
    f_odd = f_odd + 0.25 * (odd_hi.astype(jnp.float32) + odd_lo.astype(jnp.float32))
    f_even = dot_nt(odd_hi, ghi) + dot_nt(odd_lo, ghi) + dot_nt(odd_hi, glo)
    f_even = f_even + 0.25 * (even_hi.astype(jnp.float32) + even_lo.astype(jnp.float32))
    fe = f_even.astype(jnp.bfloat16)
    fo = f_odd.astype(jnp.bfloat16)
    permt = permt_ref[...]
    nat = []
    for b in range(nblk):
        pair = jnp.concatenate([fe[:, b * hb:(b + 1) * hb], fo[:, b * hb:(b + 1) * hb]], axis=1)
        nat.append(dot(pair, permt))
    filtered = jnp.concatenate(nat, axis=1)

    pad_cols = fs_scr.shape[1] - col_count
    fs_scr[:, col_count:] = jnp.zeros((row_count, pad_cols), jnp.float32)
    w_iota = lax.broadcasted_iota(jnp.int32, (2 * TILE, TILE), 0)
    i_iota = lax.broadcasted_iota(jnp.int32, (1, TILE), 1)
    span = 3 * TILE
    for q in range(GROUP):
        p = g * GROUP + q
        stretch_one = st_ref[p]
        offset_one = off_ref[p]
        tilt_one = tilt_ref[p]
        fs_scr[:, :col_count] = filtered[q * row_count:(q + 1) * row_count, :]
        scaled = i_iota * stretch_one
        rel = scaled // TILE
        frac = (scaled % TILE).astype(jnp.float32) / TILE
        hat = jnp.where(w_iota == rel, 1.0 - frac, 0.0) + jnp.where(w_iota == rel + 1, frac, 0.0)
        windows = []
        for t in range(tile_count):
            lo_col = t * stretch_one + offset_one
            blk_id = lo_col // TILE
            start = pl.multiple_of(blk_id * TILE, TILE)
            near = fs_scr[:, pl.ds(start, span)]
            moved = pltpu.roll(near, (span - (lo_col - blk_id * TILE)) % span, 1)
            windows.append(moved[:, :2 * TILE].astype(jnp.bfloat16))
        img = dot(jnp.concatenate(windows, axis=0), hat.astype(jnp.bfloat16))
        image = jnp.concatenate(
            [img[t * row_count:(t + 1) * row_count] for t in range(tile_count)], axis=1
        )
        base = pl.multiple_of((tilt_one // 8) * 8, 8)
        padded = jnp.concatenate([image, jnp.zeros((8, col_count), jnp.float32)], axis=0)
        acc_scr[pl.ds(base, row_count + 8), :] += pltpu.roll(padded, tilt_one % 8, 0)

    @pl.when(g == pl.num_programs(0) - 1)
    def _():
        parts, own_rows, width = own_ref.shape
        layer_rows = own_rows + out_ref.shape[1]
        me = me_ref[0]
        for pos in range(parts):
            c0 = pl.multiple_of((me ^ pos) * width, TILE)
            own_ref[pos] = acc_scr[:own_rows, pl.ds(c0, width)]
            out_ref[pos] = acc_scr[own_rows:layer_rows, pl.ds(c0, width)]


def deposit(flat_weights, stretch, offset, tilt_shift, projections, mean_flat, eigen_flats, parts, me):
    proj_count, row_count, col_count = projections.shape
    flat_count = eigen_flats.shape[0]
    half = col_count // 2
    ghi, glo = half_table(half)
    perm, permt = block_perm()
    smem = pl.BlockSpec(memory_space=pltpu.SMEM)
    once = dict(pipeline_mode=pl.Buffered(1))
    return pl.pallas_call(
        main_kernel,
        grid=(proj_count // GROUP,),
        in_specs=[
            smem, smem, smem, smem,
            pl.BlockSpec((GROUP, row_count, col_count), lambda g: (g, 0, 0)),
            pl.BlockSpec((row_count, col_count), lambda g: (0, 0), **once),
            pl.BlockSpec(memory_space=pl.ANY),
            pl.BlockSpec(memory_space=pl.ANY),
            pl.BlockSpec(memory_space=pl.ANY),
            pl.BlockSpec((BLK, BLK), lambda g: (0, 0), **once),
            pl.BlockSpec((BLK, BLK), lambda g: (0, 0), **once),
            smem,
        ],
        out_specs=[
            pl.BlockSpec((parts, row_count, col_count // parts), lambda g: (0, 0, 0)),
            pl.BlockSpec((parts, 2 * row_count, col_count // parts), lambda g: (0, 0, 0)),
        ],
        out_shape=[
            jax.ShapeDtypeStruct((parts, row_count, col_count // parts), jnp.float32),
            jax.ShapeDtypeStruct((parts, 2 * row_count, col_count // parts), jnp.float32),
        ],
        scratch_shapes=[
            pltpu.VMEM((GROUP * row_count, col_count), jnp.float32),
            pltpu.VMEM((row_count, col_count + 2 * TILE), jnp.float32),
            pltpu.VMEM((3 * row_count + 8, col_count), jnp.float32),
            pltpu.VMEM((flat_count, row_count, col_count), jnp.float32),
            pltpu.VMEM((half, half), jnp.bfloat16),
            pltpu.VMEM((half, half), jnp.bfloat16),
            pltpu.SemaphoreType.DMA((row_count // CHUNK + 1, max(flat_count, 2))),
        ],
        compiler_params=pltpu.CompilerParams(
            dimension_semantics=("arbitrary",), vmem_limit_bytes=60 * 1024 * 1024
        ),
    )(flat_weights, stretch, offset, tilt_shift, projections, mean_flat, eigen_flats, ghi, glo, perm, permt, me)


def all_sum(value, axis):
    size = lax.axis_size(axis)
    if size & (size - 1):
        total = value
        for by in range(1, size):
            total = total + lax.ppermute(value, axis, [(i, (i + by) % size) for i in range(size)])
        return total
    by = 1
    while by < size:
        value = value + lax.ppermute(value, axis, [(i, i ^ by) for i in range(size)])
        by *= 2
    return value


def gram_kernel(e_ref, p_ref, m_ref, o_ref, x_scr):
    flat_count, block_rows, _ = e_ref.shape
    proj_count = p_ref.shape[0]

    @pl.when(pl.program_id(0) == 0)
    def _():
        x_scr[...] = jnp.zeros_like(x_scr)
        o_ref[...] = jnp.zeros_like(o_ref)

    acc = o_ref[...]
    for r in range(0, block_rows, STRIDE):
        mean_row = m_ref[pl.ds(r, 1), :]
        for k in range(flat_count):
            x_scr[pl.ds(k, 1), :] = e_ref[k, pl.ds(r, 1), :]
        for p in range(proj_count):
            x_scr[pl.ds(flat_count + p, 1), :] = p_ref[p, pl.ds(r, 1), :] - mean_row
        xs = x_scr[...]
        acc = acc + lax.dot_general(
            xs, xs, (((1,), (1,)), ((), ())),
            precision=lax.Precision.HIGHEST, preferred_element_type=jnp.float32,
        )
    o_ref[...] = acc


def sampled_gram(projections, mean_flat, eigen_flats):
    proj_count, row_count, col_count = projections.shape
    flat_count = eigen_flats.shape[0]
    width = -(-(flat_count + proj_count) // 8) * 8
    block_rows = math.gcd(32, row_count)
    return pl.pallas_call(
        gram_kernel,
        grid=(row_count // block_rows,),
        in_specs=[
            pl.BlockSpec((flat_count, block_rows, col_count), lambda i: (0, i, 0)),
            pl.BlockSpec((proj_count, block_rows, col_count), lambda i: (0, i, 0)),
            pl.BlockSpec((block_rows, col_count), lambda i: (i, 0)),
        ],
        out_specs=pl.BlockSpec((width, width), lambda i: (0, 0)),
        out_shape=jax.ShapeDtypeStruct((width, width), jnp.float32),
        scratch_shapes=[pltpu.VMEM((width, col_count), jnp.float32)],
        compiler_params=pltpu.CompilerParams(dimension_semantics=("arbitrary",)),
    )(eigen_flats, projections, mean_flat)


def scatter_sum(chunks, axis):
    size, rows, width = chunks.shape
    current = chunks
    level = 0
    while current.shape[0] > 1:
        pairs = current.reshape(current.shape[0] // 2, 2, rows, width)
        got = lax.ppermute(pairs[:, 1], axis, [(i, i ^ (1 << level)) for i in range(size)])
        current = pairs[:, 0] + got
        level += 1
    return current[0]


def per_device(projections, mean_flat, eigen_flats, stretch, offset, tilt_shift):
    proj_count, row_count, col_count = projections.shape
    flat_count = eigen_flats.shape[0]
    total_proj = proj_count * lax.axis_size("angle")
    gram_part = sampled_gram(projections, mean_flat, eigen_flats)
    gram_all = all_sum(gram_part, "row")
    gram_matrix = gram_all[:flat_count, :flat_count]
    rhs_matrix = gram_all[:flat_count, flat_count:flat_count + proj_count]
    gram_matrix = gram_matrix + col_count * jnp.eye(flat_count, dtype=jnp.float32)
    cholesky_factor = jnp.linalg.cholesky(gram_matrix)
    middle = lax.linalg.triangular_solve(cholesky_factor, rhs_matrix, left_side=True, lower=True)
    solved = lax.linalg.triangular_solve(
        cholesky_factor, middle, left_side=True, lower=True, transpose_a=True
    )
    flat_weights = solved.T
    angle_count = lax.axis_size("angle")
    if angle_count & (angle_count - 1):
        own, moving = deposit(
            flat_weights, stretch, offset, tilt_shift, projections, mean_flat, eigen_flats,
            1, jnp.zeros((1,), jnp.int32),
        )
        own = lax.psum_scatter(own[0], "angle", scatter_dimension=1, tiled=True)
        moving = lax.psum_scatter(moving[0], "angle", scatter_dimension=1, tiled=True)
    else:
        me = lax.axis_index("angle").astype(jnp.int32).reshape(1)
        own, moving = deposit(
            flat_weights, stretch, offset, tilt_shift, projections, mean_flat, eigen_flats,
            angle_count, me,
        )
        moving = scatter_sum(moving, "angle")
        own = scatter_sum(own, "angle")
    from_next = shifted(moving[:row_count], "row", 1)
    from_second = shifted(moving[row_count:], "row", 2)
    summed = own + from_next + from_second
    return summed / math.sqrt(total_proj)


def solution(mesh):
    return jax.shard_map(
        per_device,
        mesh=mesh,
        in_specs=(
            P("angle", "row", None),
            P("row", None),
            P(None, "row", None),
            P("angle"),
            P("angle"),
            P("angle"),
        ),
        out_specs=P("row", "angle"),
        check_vma=False,
    )
```

```python
import math

import jax
import jax.numpy as jnp
from jax import lax
from jax.experimental import pallas as pl
from jax.experimental.pallas import tpu as pltpu
from jax.sharding import PartitionSpec as P

TILE = 128
STRIDE = 4
GROUP = 4
BLK = 256
CHUNK = 16


def shifted(value, axis, by):
    size = lax.axis_size(axis)
    pairs = [(i, i + by) for i in range(size) if 0 <= i + by < size]
    return lax.ppermute(value, axis, pairs)


def split_bf16(x):
    hi = x.astype(jnp.bfloat16)
    lo = (x - hi.astype(jnp.float32)).astype(jnp.bfloat16)
    return hi, lo


def half_table(half):
    idx = lax.optimization_barrier(jnp.arange(half, dtype=jnp.int32))
    dist = (2 * (idx[None, :] - idx[:, None]) + 1).astype(jnp.float32)
    table = -1.0 / (math.pi * math.pi * dist * dist)
    return split_bf16(table)


def block_perm():
    rows = jnp.arange(BLK, dtype=jnp.int32)[:, None]
    cols = jnp.arange(BLK, dtype=jnp.int32)[None, :]
    target = rows // 2 + (BLK // 2) * (rows % 2)
    perm = (cols == target).astype(jnp.bfloat16)
    return perm, perm.T


def dot(a, b):
    return jnp.dot(a, b, preferred_element_type=jnp.float32)


def dot_nt(a, b):
    return lax.dot_general(a, b, (((1,), (1,)), ((), ())), preferred_element_type=jnp.float32)


def main_kernel(w_ref, st_ref, off_ref, tilt_ref, proj_ref, mean_ref, e_hbm, ghi_hbm, glo_hbm,
                perm_ref, permt_ref, me_ref, own_keep, own_give, out_keep, out_give, a_scr, fs_scr, acc_scr,
                e_ref, ghi_ref, glo_ref, sem):
    g = pl.program_id(0)
    flat_count, row_count, col_count = e_ref.shape
    chunks = row_count // CHUNK

    def slab_copy(c, k):
        rows_c = pl.ds(pl.multiple_of(c * CHUNK, CHUNK), CHUNK)
        return pltpu.make_async_copy(e_hbm.at[k, rows_c, :], e_ref.at[k, rows_c, :], sem.at[c, k])

    table_copies = [
        pltpu.make_async_copy(ghi_hbm, ghi_ref, sem.at[chunks, 0]),
        pltpu.make_async_copy(glo_hbm, glo_ref, sem.at[chunks, 1]),
    ]

    @pl.when(g == 0)
    def _():
        for c in range(chunks):
            for k in range(flat_count):
                slab_copy(c, k).start()
        for copy in table_copies:
            copy.start()
    rows = GROUP * row_count
    half = col_count // 2
    nblk = col_count // BLK
    hb = BLK // 2
    tile_count = col_count // TILE

    @pl.when(g == 0)
    def _():
        acc_scr[...] = jnp.zeros_like(acc_scr)

    weights = [[w_ref[g * GROUP + q, k] for k in range(flat_count)] for q in range(GROUP)]

    def absorb_chunk(c, carry):
        @pl.when(g == 0)
        def _():
            for k in range(flat_count):
                slab_copy(c, k).wait()

        r0 = pl.multiple_of(c * CHUNK, CHUNK)
        mean_rows = mean_ref[pl.ds(r0, CHUNK), :]
        for q in range(GROUP):
            acc = mean_rows - proj_ref[q, pl.ds(r0, CHUNK), :]
            for k in range(flat_count):
                acc = acc + weights[q][k] * e_ref[k, pl.ds(r0, CHUNK), :]
            a_scr[pl.ds(q * row_count + r0, CHUNK), :] = acc
        return carry

    lax.fori_loop(0, chunks, absorb_chunk, 0)

    @pl.when(g == 0)
    def _():
        for copy in table_copies:
            copy.wait()

    perm = perm_ref[...]
    even_hi, even_lo, odd_hi, odd_lo = [], [], [], []
    for b in range(nblk):
        blk = a_scr[:, b * BLK:(b + 1) * BLK]
        hi, lo = split_bf16(blk)
        ph = dot(hi, perm).astype(jnp.bfloat16)
        po = dot(lo, perm).astype(jnp.bfloat16)
        even_hi.append(ph[:, :hb])
        odd_hi.append(ph[:, hb:])
        even_lo.append(po[:, :hb])
        odd_lo.append(po[:, hb:])
    even_hi = jnp.concatenate(even_hi, axis=1)
    even_lo = jnp.concatenate(even_lo, axis=1)
    odd_hi = jnp.concatenate(odd_hi, axis=1)
    odd_lo = jnp.concatenate(odd_lo, axis=1)
    ghi = ghi_ref[...]
    glo = glo_ref[...]
    f_odd = dot(even_hi, ghi) + dot(even_lo, ghi) + dot(even_hi, glo)
    f_odd = f_odd + 0.25 * (odd_hi.astype(jnp.float32) + odd_lo.astype(jnp.float32))
    f_even = dot_nt(odd_hi, ghi) + dot_nt(odd_lo, ghi) + dot_nt(odd_hi, glo)
    f_even = f_even + 0.25 * (even_hi.astype(jnp.float32) + even_lo.astype(jnp.float32))
    fe = f_even.astype(jnp.bfloat16)
    fo = f_odd.astype(jnp.bfloat16)
    permt = permt_ref[...]
    nat = []
    for b in range(nblk):
        pair = jnp.concatenate([fe[:, b * hb:(b + 1) * hb], fo[:, b * hb:(b + 1) * hb]], axis=1)
        nat.append(dot(pair, permt))
    filtered = jnp.concatenate(nat, axis=1)

    pad_cols = fs_scr.shape[1] - col_count
    fs_scr[:, col_count:] = jnp.zeros((row_count, pad_cols), jnp.float32)
    w_iota = lax.broadcasted_iota(jnp.int32, (2 * TILE, TILE), 0)
    i_iota = lax.broadcasted_iota(jnp.int32, (1, TILE), 1)
    span = 3 * TILE
    for q in range(GROUP):
        p = g * GROUP + q
        stretch_one = st_ref[p]
        offset_one = off_ref[p]
        tilt_one = tilt_ref[p]
        fs_scr[:, :col_count] = filtered[q * row_count:(q + 1) * row_count, :]
        scaled = i_iota * stretch_one
        rel = scaled // TILE
        frac = (scaled % TILE).astype(jnp.float32) / TILE
        hat = jnp.where(w_iota == rel, 1.0 - frac, 0.0) + jnp.where(w_iota == rel + 1, frac, 0.0)
        windows = []
        for t in range(tile_count):
            lo_col = t * stretch_one + offset_one
            blk_id = lo_col // TILE
            start = pl.multiple_of(blk_id * TILE, TILE)
            near = fs_scr[:, pl.ds(start, span)]
            moved = pltpu.roll(near, (span - (lo_col - blk_id * TILE)) % span, 1)
            windows.append(moved[:, :2 * TILE].astype(jnp.bfloat16))
        img = dot(jnp.concatenate(windows, axis=0), hat.astype(jnp.bfloat16))
        image = jnp.concatenate(
            [img[t * row_count:(t + 1) * row_count] for t in range(tile_count)], axis=1
        )
        base = pl.multiple_of((tilt_one // 8) * 8, 8)
        padded = jnp.concatenate([image, jnp.zeros((8, col_count), jnp.float32)], axis=0)
        acc_scr[pl.ds(base, row_count + 8), :] += pltpu.roll(padded, tilt_one % 8, 0)

    @pl.when(g == pl.num_programs(0) - 1)
    def _():
        halves, own_rows, width = own_keep.shape
        parts = col_count // width
        layer_rows = own_rows + out_keep.shape[1]
        me = me_ref[0]
        bits = parts.bit_length() - 1
        for idx in range(parts):
            pos = int(format(idx, "b").zfill(bits)[::-1], 2) if bits else 0
            c0 = pl.multiple_of((me ^ pos) * width, TILE)
            own_ref, out_ref, at = (own_keep, out_keep, idx) if idx < halves else (own_give, out_give, idx - halves)
            own_ref[at] = acc_scr[:own_rows, pl.ds(c0, width)]
            out_ref[at] = acc_scr[own_rows:layer_rows, pl.ds(c0, width)]


def deposit(flat_weights, stretch, offset, tilt_shift, projections, mean_flat, eigen_flats, parts, me):
    proj_count, row_count, col_count = projections.shape
    flat_count = eigen_flats.shape[0]
    half = col_count // 2
    ghi, glo = half_table(half)
    perm, permt = block_perm()
    smem = pl.BlockSpec(memory_space=pltpu.SMEM)
    once = dict(pipeline_mode=pl.Buffered(1))
    halves = max(parts // 2, 1)
    return pl.pallas_call(
        main_kernel,
        grid=(proj_count // GROUP,),
        in_specs=[
            smem, smem, smem, smem,
            pl.BlockSpec((GROUP, row_count, col_count), lambda g: (g, 0, 0)),
            pl.BlockSpec((row_count, col_count), lambda g: (0, 0), **once),
            pl.BlockSpec(memory_space=pl.ANY),
            pl.BlockSpec(memory_space=pl.ANY),
            pl.BlockSpec(memory_space=pl.ANY),
            pl.BlockSpec((BLK, BLK), lambda g: (0, 0), **once),
            pl.BlockSpec((BLK, BLK), lambda g: (0, 0), **once),
            smem,
        ],
        out_specs=[
            pl.BlockSpec((halves, rows_out, col_count // parts), lambda g: (0, 0, 0))
            for rows_out in (row_count, row_count, 2 * row_count, 2 * row_count)
        ],
        out_shape=[
            jax.ShapeDtypeStruct((halves, rows_out, col_count // parts), jnp.float32)
            for rows_out in (row_count, row_count, 2 * row_count, 2 * row_count)
        ],
        scratch_shapes=[
            pltpu.VMEM((GROUP * row_count, col_count), jnp.float32),
            pltpu.VMEM((row_count, col_count + 2 * TILE), jnp.float32),
            pltpu.VMEM((3 * row_count + 8, col_count), jnp.float32),
            pltpu.VMEM((flat_count, row_count, col_count), jnp.float32),
            pltpu.VMEM((half, half), jnp.bfloat16),
            pltpu.VMEM((half, half), jnp.bfloat16),
            pltpu.SemaphoreType.DMA((row_count // CHUNK + 1, max(flat_count, 2))),
        ],
        compiler_params=pltpu.CompilerParams(
            dimension_semantics=("arbitrary",), vmem_limit_bytes=60 * 1024 * 1024
        ),
    )(flat_weights, stretch, offset, tilt_shift, projections, mean_flat, eigen_flats, ghi, glo, perm, permt, me)


def all_sum(value, axis):
    size = lax.axis_size(axis)
    if size & (size - 1):
        total = value
        for by in range(1, size):
            total = total + lax.ppermute(value, axis, [(i, (i + by) % size) for i in range(size)])
        return total
    by = 1
    while by < size:
        value = value + lax.ppermute(value, axis, [(i, i ^ by) for i in range(size)])
        by *= 2
    return value


def gram_kernel(e_ref, p_ref, m_ref, o_ref, x_scr):
    flat_count, block_rows, _ = e_ref.shape
    proj_count = p_ref.shape[0]

    @pl.when(pl.program_id(0) == 0)
    def _():
        x_scr[...] = jnp.zeros_like(x_scr)
        o_ref[...] = jnp.zeros_like(o_ref)

    acc = o_ref[...]
    for r in range(0, block_rows, STRIDE):
        mean_row = m_ref[pl.ds(r, 1), :]
        for k in range(flat_count):
            x_scr[pl.ds(k, 1), :] = e_ref[k, pl.ds(r, 1), :]
        for p in range(proj_count):
            x_scr[pl.ds(flat_count + p, 1), :] = p_ref[p, pl.ds(r, 1), :] - mean_row
        xs = x_scr[...]
        acc = acc + lax.dot_general(
            xs, xs, (((1,), (1,)), ((), ())),
            precision=lax.Precision.HIGHEST, preferred_element_type=jnp.float32,
        )
    o_ref[...] = acc


def sampled_gram(projections, mean_flat, eigen_flats):
    proj_count, row_count, col_count = projections.shape
    flat_count = eigen_flats.shape[0]
    width = -(-(flat_count + proj_count) // 8) * 8
    block_rows = math.gcd(32, row_count)
    return pl.pallas_call(
        gram_kernel,
        grid=(row_count // block_rows,),
        in_specs=[
            pl.BlockSpec((flat_count, block_rows, col_count), lambda i: (0, i, 0)),
            pl.BlockSpec((proj_count, block_rows, col_count), lambda i: (0, i, 0)),
            pl.BlockSpec((block_rows, col_count), lambda i: (i, 0)),
        ],
        out_specs=pl.BlockSpec((width, width), lambda i: (0, 0)),
        out_shape=jax.ShapeDtypeStruct((width, width), jnp.float32),
        scratch_shapes=[pltpu.VMEM((width, col_count), jnp.float32)],
        compiler_params=pltpu.CompilerParams(dimension_semantics=("arbitrary",)),
    )(eigen_flats, projections, mean_flat)


def scatter_sum(keep, give, axis):
    size = 2 * keep.shape[0]
    current = keep + lax.ppermute(give, axis, [(i, i ^ 1) for i in range(size)])
    level = 1
    while current.shape[0] > 1:
        half = current.shape[0] // 2
        got = lax.ppermute(current[half:], axis, [(i, i ^ (1 << level)) for i in range(size)])
        current = current[:half] + got
        level += 1
    return current[0]


def per_device(projections, mean_flat, eigen_flats, stretch, offset, tilt_shift):
    proj_count, row_count, col_count = projections.shape
    flat_count = eigen_flats.shape[0]
    total_proj = proj_count * lax.axis_size("angle")
    gram_part = sampled_gram(projections, mean_flat, eigen_flats)
    gram_all = all_sum(gram_part, "row")
    gram_matrix = gram_all[:flat_count, :flat_count]
    rhs_matrix = gram_all[:flat_count, flat_count:flat_count + proj_count]
    gram_matrix = gram_matrix + col_count * jnp.eye(flat_count, dtype=jnp.float32)
    cholesky_factor = jnp.linalg.cholesky(gram_matrix)
    middle = lax.linalg.triangular_solve(cholesky_factor, rhs_matrix, left_side=True, lower=True)
    solved = lax.linalg.triangular_solve(
        cholesky_factor, middle, left_side=True, lower=True, transpose_a=True
    )
    flat_weights = solved.T
    angle_count = lax.axis_size("angle")
    if angle_count & (angle_count - 1):
        own, _, moving, _ = deposit(
            flat_weights, stretch, offset, tilt_shift, projections, mean_flat, eigen_flats,
            1, jnp.zeros((1,), jnp.int32),
        )
        own = lax.psum_scatter(own[0], "angle", scatter_dimension=1, tiled=True)
        moving = lax.psum_scatter(moving[0], "angle", scatter_dimension=1, tiled=True)
    else:
        me = lax.axis_index("angle").astype(jnp.int32).reshape(1)
        own_keep, own_give, moving_keep, moving_give = deposit(
            flat_weights, stretch, offset, tilt_shift, projections, mean_flat, eigen_flats,
            angle_count, me,
        )
        moving = scatter_sum(moving_keep, moving_give, "angle")
        own = scatter_sum(own_keep, own_give, "angle")
    from_next = shifted(moving[:row_count], "row", 1)
    from_second = shifted(moving[row_count:], "row", 2)
    summed = own + from_next + from_second
    return summed / math.sqrt(total_proj)


def solution(mesh):
    return jax.shard_map(
        per_device,
        mesh=mesh,
        in_specs=(
            P("angle", "row", None),
            P("row", None),
            P(None, "row", None),
            P("angle"),
            P("angle"),
            P("angle"),
        ),
        out_specs=P("row", "angle"),
        check_vma=False,
    )
```

```python
import functools
import math

import jax
import jax.numpy as jnp
from jax import lax
from jax.experimental import pallas as pl
from jax.experimental.pallas import tpu as pltpu
from jax.sharding import PartitionSpec as P

TILE = 128
STRIDE = 4
GROUP = 4
BLK = 256
CHUNK = 16


def shifted(value, axis, by):
    size = lax.axis_size(axis)
    pairs = [(i, i + by) for i in range(size) if 0 <= i + by < size]
    return lax.ppermute(value, axis, pairs)


def split_bf16(x):
    hi = x.astype(jnp.bfloat16)
    lo = (x - hi.astype(jnp.float32)).astype(jnp.bfloat16)
    return hi, lo


def half_table(half):
    idx = lax.optimization_barrier(jnp.arange(half, dtype=jnp.int32))
    dist = (2 * (idx[None, :] - idx[:, None]) + 1).astype(jnp.float32)
    table = -1.0 / (math.pi * math.pi * dist * dist)
    return split_bf16(table)


def block_perm():
    rows = jnp.arange(BLK, dtype=jnp.int32)[:, None]
    cols = jnp.arange(BLK, dtype=jnp.int32)[None, :]
    target = rows // 2 + (BLK // 2) * (rows % 2)
    perm = (cols == target).astype(jnp.bfloat16)
    return perm, perm.T


def dot(a, b):
    return jnp.dot(a, b, preferred_element_type=jnp.float32)


def dot_nt(a, b):
    return lax.dot_general(a, b, (((1,), (1,)), ((), ())), preferred_element_type=jnp.float32)


def main_kernel(w_ref, st_ref, off_ref, tilt_ref, proj_ref, mean_ref, e_hbm, ghi_hbm, glo_hbm,
                perm_ref, permt_ref, me_ref, own_keep, own_give, out_keep, out_give, a_scr, fs_scr, acc_scr,
                e_ref, ghi_ref, glo_ref, sem):
    g = pl.program_id(0)
    flat_count, row_count, col_count = e_ref.shape
    chunks = row_count // CHUNK

    def slab_copy(c, k):
        rows_c = pl.ds(pl.multiple_of(c * CHUNK, CHUNK), CHUNK)
        return pltpu.make_async_copy(e_hbm.at[k, rows_c, :], e_ref.at[k, rows_c, :], sem.at[c, k])

    table_copies = [
        pltpu.make_async_copy(ghi_hbm, ghi_ref, sem.at[chunks, 0]),
        pltpu.make_async_copy(glo_hbm, glo_ref, sem.at[chunks, 1]),
    ]

    @pl.when(g == 0)
    def _():
        for c in range(chunks):
            for k in range(flat_count):
                slab_copy(c, k).start()
        for copy in table_copies:
            copy.start()
    rows = GROUP * row_count
    half = col_count // 2
    nblk = col_count // BLK
    hb = BLK // 2
    tile_count = col_count // TILE

    @pl.when(g == 0)
    def _():
        acc_scr[...] = jnp.zeros_like(acc_scr)

    weights = [[w_ref[k, flat_count + g * GROUP + q] for k in range(flat_count)] for q in range(GROUP)]

    def absorb_chunk(c, carry):
        @pl.when(g == 0)
        def _():
            for k in range(flat_count):
                slab_copy(c, k).wait()

        r0 = pl.multiple_of(c * CHUNK, CHUNK)
        mean_rows = mean_ref[pl.ds(r0, CHUNK), :]
        for q in range(GROUP):
            acc = mean_rows - proj_ref[q, pl.ds(r0, CHUNK), :]
            for k in range(flat_count):
                acc = acc + weights[q][k] * e_ref[k, pl.ds(r0, CHUNK), :]
            a_scr[pl.ds(q * row_count + r0, CHUNK), :] = acc
        return carry

    lax.fori_loop(0, chunks, absorb_chunk, 0)

    @pl.when(g == 0)
    def _():
        for copy in table_copies:
            copy.wait()

    perm = perm_ref[...]
    even_hi, even_lo, odd_hi, odd_lo = [], [], [], []
    for b in range(nblk):
        blk = a_scr[:, b * BLK:(b + 1) * BLK]
        hi, lo = split_bf16(blk)
        ph = dot(hi, perm).astype(jnp.bfloat16)
        po = dot(lo, perm).astype(jnp.bfloat16)
        even_hi.append(ph[:, :hb])
        odd_hi.append(ph[:, hb:])
        even_lo.append(po[:, :hb])
        odd_lo.append(po[:, hb:])
    even_hi = jnp.concatenate(even_hi, axis=1)
    even_lo = jnp.concatenate(even_lo, axis=1)
    odd_hi = jnp.concatenate(odd_hi, axis=1)
    odd_lo = jnp.concatenate(odd_lo, axis=1)
    ghi = ghi_ref[...]
    glo = glo_ref[...]
    f_odd = dot(even_hi, ghi) + dot(even_lo, ghi) + dot(even_hi, glo)
    f_odd = f_odd + 0.25 * (odd_hi.astype(jnp.float32) + odd_lo.astype(jnp.float32))
    f_even = dot_nt(odd_hi, ghi) + dot_nt(odd_lo, ghi) + dot_nt(odd_hi, glo)
    f_even = f_even + 0.25 * (even_hi.astype(jnp.float32) + even_lo.astype(jnp.float32))
    fe = f_even.astype(jnp.bfloat16)
    fo = f_odd.astype(jnp.bfloat16)
    permt = permt_ref[...]
    nat = []
    for b in range(nblk):
        pair = jnp.concatenate([fe[:, b * hb:(b + 1) * hb], fo[:, b * hb:(b + 1) * hb]], axis=1)
        nat.append(dot(pair, permt))
    filtered = jnp.concatenate(nat, axis=1)

    pad_cols = fs_scr.shape[1] - col_count
    fs_scr[:, col_count:] = jnp.zeros((row_count, pad_cols), jnp.float32)
    w_iota = lax.broadcasted_iota(jnp.int32, (2 * TILE, TILE), 0)
    i_iota = lax.broadcasted_iota(jnp.int32, (1, TILE), 1)
    span = 3 * TILE
    for q in range(GROUP):
        p = g * GROUP + q
        stretch_one = st_ref[p]
        offset_one = off_ref[p]
        tilt_one = tilt_ref[p]
        fs_scr[:, :col_count] = filtered[q * row_count:(q + 1) * row_count, :]
        scaled = i_iota * stretch_one
        rel = scaled // TILE
        frac = (scaled % TILE).astype(jnp.float32) / TILE
        hat = jnp.where(w_iota == rel, 1.0 - frac, 0.0) + jnp.where(w_iota == rel + 1, frac, 0.0)
        windows = []
        for t in range(tile_count):
            lo_col = t * stretch_one + offset_one
            blk_id = lo_col // TILE
            start = pl.multiple_of(blk_id * TILE, TILE)
            near = fs_scr[:, pl.ds(start, span)]
            moved = pltpu.roll(near, (span - (lo_col - blk_id * TILE)) % span, 1)
            windows.append(moved[:, :2 * TILE].astype(jnp.bfloat16))
        img = dot(jnp.concatenate(windows, axis=0), hat.astype(jnp.bfloat16))
        image = jnp.concatenate(
            [img[t * row_count:(t + 1) * row_count] for t in range(tile_count)], axis=1
        )
        base = pl.multiple_of((tilt_one // 8) * 8, 8)
        padded = jnp.concatenate([image, jnp.zeros((8, col_count), jnp.float32)], axis=0)
        acc_scr[pl.ds(base, row_count + 8), :] += pltpu.roll(padded, tilt_one % 8, 0)

    @pl.when(g == pl.num_programs(0) - 1)
    def _():
        halves, own_rows, width = own_keep.shape
        parts = col_count // width
        layer_rows = own_rows + out_keep.shape[1]
        me = me_ref[0]
        bits = parts.bit_length() - 1
        for idx in range(parts):
            pos = int(format(idx, "b").zfill(bits)[::-1], 2) if bits else 0
            c0 = pl.multiple_of((me ^ pos) * width, TILE)
            own_ref, out_ref, at = (own_keep, out_keep, idx) if idx < halves else (own_give, out_give, idx - halves)
            own_ref[at] = acc_scr[:own_rows, pl.ds(c0, width)]
            out_ref[at] = acc_scr[own_rows:layer_rows, pl.ds(c0, width)]


def deposit(flat_weights, stretch, offset, tilt_shift, projections, mean_flat, eigen_flats, parts, me):
    proj_count, row_count, col_count = projections.shape
    flat_count = eigen_flats.shape[0]
    half = col_count // 2
    ghi, glo = half_table(half)
    perm, permt = block_perm()
    smem = pl.BlockSpec(memory_space=pltpu.SMEM)
    once = dict(pipeline_mode=pl.Buffered(1))
    halves = max(parts // 2, 1)
    return pl.pallas_call(
        main_kernel,
        grid=(proj_count // GROUP,),
        in_specs=[
            smem, smem, smem, smem,
            pl.BlockSpec((GROUP, row_count, col_count), lambda g: (g, 0, 0)),
            pl.BlockSpec((row_count, col_count), lambda g: (0, 0), **once),
            pl.BlockSpec(memory_space=pl.ANY),
            pl.BlockSpec(memory_space=pl.ANY),
            pl.BlockSpec(memory_space=pl.ANY),
            pl.BlockSpec((BLK, BLK), lambda g: (0, 0), **once),
            pl.BlockSpec((BLK, BLK), lambda g: (0, 0), **once),
            smem,
        ],
        out_specs=[
            pl.BlockSpec((halves, rows_out, col_count // parts), lambda g: (0, 0, 0))
            for rows_out in (row_count, row_count, 2 * row_count, 2 * row_count)
        ],
        out_shape=[
            jax.ShapeDtypeStruct((halves, rows_out, col_count // parts), jnp.float32)
            for rows_out in (row_count, row_count, 2 * row_count, 2 * row_count)
        ],
        scratch_shapes=[
            pltpu.VMEM((GROUP * row_count, col_count), jnp.float32),
            pltpu.VMEM((row_count, col_count + 2 * TILE), jnp.float32),
            pltpu.VMEM((3 * row_count + 8, col_count), jnp.float32),
            pltpu.VMEM((flat_count, row_count, col_count), jnp.float32),
            pltpu.VMEM((half, half), jnp.bfloat16),
            pltpu.VMEM((half, half), jnp.bfloat16),
            pltpu.SemaphoreType.DMA((row_count // CHUNK + 1, max(flat_count, 2))),
        ],
        compiler_params=pltpu.CompilerParams(
            dimension_semantics=("arbitrary",), vmem_limit_bytes=60 * 1024 * 1024
        ),
    )(flat_weights, stretch, offset, tilt_shift, projections, mean_flat, eigen_flats, ghi, glo, perm, permt, me)


def all_sum(value, axis):
    size = lax.axis_size(axis)
    if size & (size - 1):
        total = value
        for by in range(1, size):
            total = total + lax.ppermute(value, axis, [(i, (i + by) % size) for i in range(size)])
        return total
    by = 1
    while by < size:
        value = value + lax.ppermute(value, axis, [(i, i ^ by) for i in range(size)])
        by *= 2
    return value


def gram_kernel(e_ref, p_ref, m_ref, o_ref, x_scr):
    flat_count, block_rows, _ = e_ref.shape
    proj_count = p_ref.shape[0]

    @pl.when(pl.program_id(0) == 0)
    def _():
        x_scr[...] = jnp.zeros_like(x_scr)
        o_ref[...] = jnp.zeros_like(o_ref)

    acc = o_ref[...]
    for r in range(0, block_rows, STRIDE):
        mean_row = m_ref[pl.ds(r, 1), :]
        for k in range(flat_count):
            x_scr[pl.ds(k, 1), :] = e_ref[k, pl.ds(r, 1), :]
        for p in range(proj_count):
            x_scr[pl.ds(flat_count + p, 1), :] = p_ref[p, pl.ds(r, 1), :] - mean_row
        xs = x_scr[...]
        acc = acc + lax.dot_general(
            xs, xs, (((1,), (1,)), ((), ())),
            precision=lax.Precision.HIGHEST, preferred_element_type=jnp.float32,
        )
    o_ref[...] = acc


def sampled_gram(projections, mean_flat, eigen_flats):
    proj_count, row_count, col_count = projections.shape
    flat_count = eigen_flats.shape[0]
    width = -(-(flat_count + proj_count) // 8) * 8
    block_rows = math.gcd(32, row_count)
    return pl.pallas_call(
        gram_kernel,
        grid=(row_count // block_rows,),
        in_specs=[
            pl.BlockSpec((flat_count, block_rows, col_count), lambda i: (0, i, 0)),
            pl.BlockSpec((proj_count, block_rows, col_count), lambda i: (0, i, 0)),
            pl.BlockSpec((block_rows, col_count), lambda i: (i, 0)),
        ],
        out_specs=pl.BlockSpec((width, width), lambda i: (0, 0)),
        out_shape=jax.ShapeDtypeStruct((width, width), jnp.float32),
        scratch_shapes=[pltpu.VMEM((width, col_count), jnp.float32)],
        compiler_params=pltpu.CompilerParams(dimension_semantics=("arbitrary",)),
    )(eigen_flats, projections, mean_flat)


def scatter_sum(keep, give, axis):
    size = 2 * keep.shape[0]
    current = keep + lax.ppermute(give, axis, [(i, i ^ 1) for i in range(size)])
    level = 1
    while current.shape[0] > 1:
        half = current.shape[0] // 2
        got = lax.ppermute(current[half:], axis, [(i, i ^ (1 << level)) for i in range(size)])
        current = current[:half] + got
        level += 1
    return current[0]


def solve_kernel(g_ref, o_ref, *, flat_count, diagonal):
    width = g_ref.shape[0]
    full = g_ref[...]
    row_i = lax.broadcasted_iota(jnp.int32, (width, width), 0)
    col_i = lax.broadcasted_iota(jnp.int32, (width, width), 1)
    rows1 = lax.broadcasted_iota(jnp.int32, (width, 1), 0)
    cols1 = lax.broadcasted_iota(jnp.int32, (1, width), 1)
    inside = (row_i < flat_count) & (col_i < flat_count)
    work = jnp.where(inside, full, 0.0) + jnp.where(inside & (row_i == col_i), diagonal, 0.0)
    rhs = jnp.where((col_i >= flat_count) & (row_i < flat_count), full, 0.0)
    lower = jnp.zeros((width, width), jnp.float32)
    upper = jnp.zeros((width, width), jnp.float32)
    for j in range(flat_count):
        col = jnp.sum(jnp.where(col_i == j, work, 0.0), axis=1, keepdims=True)
        row = jnp.sum(jnp.where(row_i == j, work, 0.0), axis=0, keepdims=True)
        pivot = jnp.sqrt(jnp.sum(jnp.where(rows1 == j, col, 0.0), axis=0, keepdims=True))
        col = jnp.where(rows1 >= j, col / pivot, 0.0)
        row = jnp.where(cols1 >= j, row / pivot, 0.0)
        lower = lower + jnp.where(col_i == j, col, 0.0)
        upper = upper + jnp.where(row_i == j, row, 0.0)
        work = work - col * row
    for j in range(flat_count):
        col = jnp.sum(jnp.where(col_i == j, lower, 0.0), axis=1, keepdims=True)
        diag = jnp.sum(jnp.where(rows1 == j, col, 0.0), axis=0, keepdims=True)
        value = jnp.sum(jnp.where(row_i == j, rhs, 0.0), axis=0, keepdims=True) / diag
        rhs = jnp.where(row_i == j, value, jnp.where(row_i > j, rhs - col * value, rhs))
    for j in reversed(range(flat_count)):
        col = jnp.sum(jnp.where(col_i == j, upper, 0.0), axis=1, keepdims=True)
        diag = jnp.sum(jnp.where(rows1 == j, col, 0.0), axis=0, keepdims=True)
        value = jnp.sum(jnp.where(row_i == j, rhs, 0.0), axis=0, keepdims=True) / diag
        rhs = jnp.where(row_i == j, value, jnp.where(row_i < j, rhs - col * value, rhs))
    o_ref[...] = rhs


def flat_solve(gram_all, flat_count, diagonal):
    width = gram_all.shape[0]
    return pl.pallas_call(
        functools.partial(solve_kernel, flat_count=flat_count, diagonal=float(diagonal)),
        out_shape=jax.ShapeDtypeStruct((width, width), jnp.float32),
    )(gram_all)


def per_device(projections, mean_flat, eigen_flats, stretch, offset, tilt_shift):
    proj_count, row_count, col_count = projections.shape
    flat_count = eigen_flats.shape[0]
    total_proj = proj_count * lax.axis_size("angle")
    gram_part = sampled_gram(projections, mean_flat, eigen_flats)
    gram_all = all_sum(gram_part, "row")
    flat_weights = flat_solve(gram_all, flat_count, col_count)
    angle_count = lax.axis_size("angle")
    if angle_count & (angle_count - 1):
        own, _, moving, _ = deposit(
            flat_weights, stretch, offset, tilt_shift, projections, mean_flat, eigen_flats,
            1, jnp.zeros((1,), jnp.int32),
        )
        own = lax.psum_scatter(own[0], "angle", scatter_dimension=1, tiled=True)
        moving = lax.psum_scatter(moving[0], "angle", scatter_dimension=1, tiled=True)
    else:
        me = lax.axis_index("angle").astype(jnp.int32).reshape(1)
        own_keep, own_give, moving_keep, moving_give = deposit(
            flat_weights, stretch, offset, tilt_shift, projections, mean_flat, eigen_flats,
            angle_count, me,
        )
        moving = scatter_sum(moving_keep, moving_give, "angle")
        own = scatter_sum(own_keep, own_give, "angle")
    from_next = shifted(moving[:row_count], "row", 1)
    from_second = shifted(moving[row_count:], "row", 2)
    summed = own + from_next + from_second
    return summed / math.sqrt(total_proj)


def solution(mesh):
    return jax.shard_map(
        per_device,
        mesh=mesh,
        in_specs=(
            P("angle", "row", None),
            P("row", None),
            P(None, "row", None),
            P("angle"),
            P("angle"),
            P("angle"),
        ),
        out_specs=P("row", "angle"),
        check_vma=False,
    )
```
